128 devices in a mesh: pipe: 4 (over x), dp: 8 (over z, y_lo), tensor: 4 (over y_hi, core).
Axes of the slice: x: 4, y: 4 (y_hi: 2, y_lo: 2; y = y_hi * 2 + y_lo), z: 4, core: 2. Of those that a mesh axis runs over, the one named last changes fastest.
Arguments:
- section_inputs: bfloat16 [4, 4096, 4096], P('pipe', ('dp', 'tensor')), may hold values from -36 to 36
- norm_gain: bfloat16 [4, 4096], P('pipe'), may hold values from 0.5 to 1.5
- query_weight: bfloat16 [4, 4096, 4096], P('pipe', None, 'tensor'), may hold values from -0.09375 to 0.09375
- key_weight: bfloat16 [4, 4096, 512], P('pipe', None, 'tensor'), may hold values from -0.09375 to 0.09375
- value_weight: bfloat16 [4, 4096, 512], P('pipe', None, 'tensor'), may hold values from -0.09375 to 0.09375
- output_weight: bfloat16 [4, 4096, 4096], P('pipe', 'tensor'), may hold values from -0.09375 to 0.09375
- upstream_grad: bfloat16 [4096, 4096], P(('dp', 'tensor')), may hold values from -6 to 6
- document_ids: int32 [8, 512], P('dp'), may hold values from 0 to 3, never falling along the last dimension, each value on 1 to 256 neighbouring positions
Outputs:
- input_grads: bfloat16 [4, 4096, 4096], P('pipe', ('dp', 'tensor'))
- query_grads: float32 [4, 4096, 4096], P('pipe', 'dp', 'tensor')
- key_grads: float32 [4, 4096, 512], P('pipe', 'dp', 'tensor')
- value_grads: float32 [4, 4096, 512], P('pipe', 'dp', 'tensor')
- output_grads: float32 [4, 4096, 4096], P('pipe', 'tensor', 'dp')
The draws below stay inside these ranges and needn't reach their ends.
Inputs may be any that keep to these rules, and one draw needn't show every extreme that they name: `document_ids`: along each sequence the document numbers never fall; each of the 4 documents holds 1 to 256 tokens, one of them exactly 256.
All inputs are finite; a program needn't handle non-finite values.
Results may differ from the reference program's by a relative error of at most 0.03.
Values may be sent and summed in bfloat16 or wider, within the bound.
No kernel may reach another device: no remote copies, remote signals or barrier semaphores. Data moves between devices by JAX's collectives and lax.ppermute only.
A program may use at most 256 MiB of HBM per device.

```python
import math
import jax
import jax.numpy as jnp
import numpy as np
from jax import lax

D = 4096
HEADS = 32
KV = 4
HD = 128
DOCS = 4
SEQ = 512
TOKENS = 4096
QW = 4096
KVW = 512
N_PIPE = 4
N_DP = 8
N_TENSOR = 4


def draw_section_inputs(key, part):
    first, second, third = jax.random.split(key, 3)
    shape = (N_PIPE, TOKENS, D)
    base = jnp.clip(jax.random.normal(first, shape, jnp.float32), -4.0, 4.0)
    row_scale = jnp.exp(jax.random.uniform(second, (N_PIPE, TOKENS, 1), jnp.float32, math.log(0.3), math.log(3.0)))
    col_scale = jnp.exp(jax.random.uniform(third, (N_PIPE, 1, D), jnp.float32, math.log(0.3), math.log(3.0)))
    return (base * row_scale * col_scale).astype(jnp.bfloat16)


def block_scale(key, dims, cuts, low, top_value):
    loudness, own = 1.0, jax.random.fold_in(key, 6)
    for axis_at, parts in cuts:
        draws = jnp.exp(jax.random.uniform(jax.random.fold_in(own, axis_at), (parts,), jnp.float32, low / len(cuts), top_value / len(cuts)))
        loudness = loudness * jnp.repeat(draws, dims[axis_at] // parts).reshape([-1 if axis == axis_at else 1 for axis in range(len(dims))])
    return loudness


def profile(count, total, most, skew):
    portions = [(1 << 20) // math.isqrt(grade ** skew) + 1 for grade in range(2, count + 1)]
    spare, counts = total - most - (count - 1), [1] * (count - 1)
    while spare > 0:
        candidates = [i for i in range(count - 1) if counts[i] < most]
        mass, remaining = sum([portions[i] for i in candidates]), spare
        for i in candidates:
            more = min(most - counts[i], max(1, remaining * portions[i] // mass), spare)
            counts[i] = counts[i] + more
            spare = spare - more
    return np.array([most] + counts)


def ragged(rng, count, total, limit, skew):
    if count == 2:
        one = jax.random.randint(rng, (), max(1, total - limit), min(limit, total - 1) + 1)
        return jnp.stack([one, total - one])
    tallies = jnp.asarray(profile(count, total, limit, skew), jnp.int32)
    pairs = (count - 1) // 2
    source_of, sink = tallies[1:1 + 2 * pairs:2], tallies[2:2 + 2 * pairs:2]
    room = jnp.minimum(source_of - 1, limit - sink)
    moved = jax.random.randint(jax.random.fold_in(rng, 1), (pairs,), 0, 1 << 20) % (room + 1)
    tallies = tallies.at[1:1 + 2 * pairs:2].set(source_of - moved).at[2:2 + 2 * pairs:2].set(sink + moved)
    return tallies[jax.random.permutation(jax.random.fold_in(rng, 2), count)]


def noise(own_key, extent, deviation, reach, shards=(), kind=jnp.bfloat16):
    values = jax.random.normal(own_key, extent, jnp.float32) * deviation
    if len(shards) > 0:
        values = block_scale(own_key, extent, shards, -0.22, 0.18) * values
    return jnp.clip(values, min=-reach, max=reach).astype(kind)


def setup_inputs(seed: int = 0) -> dict:
    arg_keys = jax.random.split(jax.random.key(seed), 9)
    return {
        "section_inputs": draw_section_inputs(jax.random.fold_in(arg_keys[8], 71), 0),
        "norm_gain": jnp.clip(1.0 + 0.1 * jax.random.normal(arg_keys[1], (N_PIPE, D), jnp.float32), 0.5, 1.5).astype(jnp.bfloat16),
        "query_weight": noise(arg_keys[2], (N_PIPE, D, QW), D ** -0.5, 0.09375, ((0, 4), (2, 4))),
        "key_weight": noise(arg_keys[3], (N_PIPE, D, KVW), D ** -0.5, 0.09375, ((0, 4), (2, 4))),
        "value_weight": noise(arg_keys[4], (N_PIPE, D, KVW), D ** -0.5, 0.09375, ((0, 4), (2, 4))),
        "output_weight": noise(arg_keys[5], (N_PIPE, QW, D), QW ** -0.5, 0.09375, ((0, 4), (1, 4))),
        "upstream_grad": noise(arg_keys[6], (TOKENS, D), 1.0, 6.0, ((0, 32),)),
        "document_ids": jax.vmap(lambda own: jnp.searchsorted(jnp.cumsum(ragged(own, DOCS, SEQ, SEQ // 2, 0)), jnp.arange(SEQ), side="right"))(jax.random.split(arg_keys[7], N_DP)).reshape((N_DP, SEQ)).astype(jnp.int32),
    }


epsilon = 1e-05
rope_base = 500000.0

def to_low(values):
    return lax.optimization_barrier(values.astype(jnp.bfloat16))

def position_tables(document_ids, head_dim):
    seq_len = document_ids.shape[1]
    index = jnp.arange(seq_len, dtype=jnp.int32)
    earlier = (document_ids[:, None, :] < document_ids[:, :, None]).astype(jnp.int32)
    position = index[None, :] - lax.optimization_barrier(jnp.sum(earlier, axis=2)).astype(jnp.int32)
    half = head_dim // 2
    expo = jnp.arange(half, dtype=jnp.float32) * (2.0 / head_dim)
    freq = jnp.exp(expo * -math.log(rope_base))
    angle = position.astype(jnp.float32)[:, :, None] * freq
    same = document_ids[:, :, None] == document_ids[:, None, :]
    causal = index[:, None] >= index[None, :]
    visible = jnp.logical_and(same, causal[None])
    return (jnp.cos(angle), jnp.sin(angle), visible)

def rotate(vector, rot_cos, rot_sin, direction):
    half = vector.shape[-1] // 2
    first = vector[..., :half]
    second = vector[..., half:]
    return jnp.concatenate([first * rot_cos - direction * second * rot_sin, second * rot_cos + direction * first * rot_sin], axis=-1)

def normalize(rows, gain):
    values = rows.astype(jnp.float32)
    inverse = lax.rsqrt(lax.optimization_barrier(jnp.mean(values * values, axis=-1, keepdims=True)) + epsilon)
    unit_rows = values * inverse
    normed = (unit_rows * gain.astype(jnp.float32)).astype(jnp.bfloat16)
    return (inverse, unit_rows, normed)

def attention_forward(query_rot, key_rot, value_low, visible):
    scale = 1.0 / math.sqrt(HD)
    scores = jnp.einsum('bqngd,bknd->bngqk', query_rot.astype(jnp.float32), key_rot.astype(jnp.float32)) * scale
    expo = jnp.where(visible[:, None, None], jnp.exp(scores), 0.0)
    prob = expo / lax.optimization_barrier(jnp.sum(expo, axis=-1, keepdims=True))
    prob_low = to_low(prob)
    mixed = jnp.einsum('bngqk,bknd->bqngd', prob_low.astype(jnp.float32), value_low.astype(jnp.float32))
    return (prob, prob_low, to_low(mixed))

def attention_backward(grad_mixed, query_rot, key_rot, value_low, prob, prob_low, rot_cos, rot_sin):
    scale = 1.0 / math.sqrt(HD)
    grad_float = grad_mixed.astype(jnp.float32)
    grad_value = jnp.einsum('bngqk,bqngd->bknd', prob_low.astype(jnp.float32), grad_float)
    grad_prob = jnp.einsum('bqngd,bknd->bngqk', grad_float, value_low.astype(jnp.float32))
    grad_score = prob * (grad_prob - lax.optimization_barrier(jnp.sum(grad_prob * prob, axis=-1, keepdims=True))) * scale
    score_low = to_low(grad_score).astype(jnp.float32)
    grad_query = jnp.einsum('bngqk,bknd->bqngd', score_low, key_rot.astype(jnp.float32))
    grad_key = jnp.einsum('bngqk,bqngd->bknd', score_low, query_rot.astype(jnp.float32))
    grad_query = rotate(grad_query, rot_cos[:, :, None, None, :], rot_sin[:, :, None, None, :], -1.0)
    grad_key = rotate(grad_key, rot_cos[:, :, None, :], rot_sin[:, :, None, :], -1.0)
    return (to_low(grad_query), to_low(grad_key), to_low(grad_value))

def back_norm(grad_normed, unit_rows, inverse, gain, incoming):
    grad_unit = grad_normed * gain.astype(jnp.float32)
    branch = (grad_unit - unit_rows * lax.optimization_barrier(jnp.mean(grad_unit * unit_rows, axis=-1, keepdims=True))) * inverse
    return (incoming.astype(jnp.float32) + branch).astype(jnp.bfloat16)

def group_sum(left, right):

    def step(total, pair):
        part = jnp.dot(pair[0].T, pair[1], preferred_element_type=jnp.float32)
        rounded = lax.optimization_barrier(part.astype(jnp.bfloat16))
        return (total + rounded.astype(jnp.float32), None)
    start = jnp.zeros((left.shape[2], right.shape[2]), jnp.float32)
    total, unused = lax.scan(step, start, (left, right))
    return total

def head_block_sum(flat_query, flat_key, flat_value, w_query, w_key, w_value):
    q_block = QW // N_TENSOR
    k_block = KVW // N_TENSOR
    total = jnp.zeros((flat_query.shape[0], D), jnp.float32)
    for block in range(N_TENSOR):
        qs = slice(block * q_block, (block + 1) * q_block)
        ks = slice(block * k_block, (block + 1) * k_block)
        partial_value = jnp.dot(flat_query[:, qs], w_query[:, qs].T, preferred_element_type=jnp.float32) + jnp.dot(flat_key[:, ks], w_key[:, ks].T, preferred_element_type=jnp.float32) + jnp.dot(flat_value[:, ks], w_value[:, ks].T, preferred_element_type=jnp.float32)
        total = total + to_low(partial_value).astype(jnp.float32)
    return total

def reference(section_inputs, norm_gain, query_weight, key_weight, value_weight, output_weight, upstream_grad, document_ids):
    groups = document_ids.shape[0]
    seq_len = document_ids.shape[1]
    group = HEADS // KV
    rot_cos, rot_sin, visible = position_tables(document_ids, HD)
    scale_out = 1.0 / math.sqrt(groups * seq_len)
    cotangent = upstream_grad.reshape(groups, seq_len, D)
    input_list = []
    query_list = []
    key_list = []
    value_list = []
    output_list = []
    for section in range(N_PIPE - 1, -1, -1):
        rows = section_inputs[section].reshape(groups, seq_len, D)
        gain = norm_gain[section]
        inverse, unit_rows, normed = normalize(rows, gain)
        flat = normed.reshape(groups * seq_len, D)
        query = jnp.dot(flat, query_weight[section], preferred_element_type=jnp.float32).reshape(groups, seq_len, KV, group, HD)
        keys = jnp.dot(flat, key_weight[section], preferred_element_type=jnp.float32).reshape(groups, seq_len, KV, HD)
        values = jnp.dot(flat, value_weight[section], preferred_element_type=jnp.float32).reshape(groups, seq_len, KV, HD)
        query_rot = to_low(rotate(query, rot_cos[:, :, None, None, :], rot_sin[:, :, None, None, :], 1.0))
        key_rot = to_low(rotate(keys, rot_cos[:, :, None, :], rot_sin[:, :, None, :], 1.0))
        value_low = to_low(values)
        prob, prob_low, mixed = attention_forward(query_rot, key_rot, value_low, visible)
        grad_mixed = to_low(jnp.dot(cotangent.reshape(groups * seq_len, D), output_weight[section].T, preferred_element_type=jnp.float32))
        grad_query, grad_key, grad_value = attention_backward(grad_mixed.reshape(groups, seq_len, KV, group, HD), query_rot, key_rot, value_low, prob, prob_low, rot_cos, rot_sin)
        flat_query = grad_query.reshape(groups * seq_len, QW)
        flat_key = grad_key.reshape(groups * seq_len, KVW)
        flat_value = grad_value.reshape(groups * seq_len, KVW)
        grad_normed = head_block_sum(flat_query, flat_key, flat_value, query_weight[section], key_weight[section], value_weight[section])
        result = back_norm(grad_normed.reshape(groups, seq_len, D), unit_rows, inverse, gain, cotangent)
        query_list.append(group_sum(normed, flat_query.reshape(groups, seq_len, QW)) * scale_out)
        key_list.append(group_sum(normed, flat_key.reshape(groups, seq_len, KVW)) * scale_out)
        value_list.append(group_sum(normed, flat_value.reshape(groups, seq_len, KVW)) * scale_out)
        output_list.append(group_sum(mixed.reshape(groups, seq_len, QW), cotangent) * scale_out)
        input_list.append(result.reshape(groups * seq_len, D))
        cotangent = result
    input_grads = jnp.stack(input_list[::-1])
    query_grads = jnp.stack(query_list[::-1])
    key_grads = jnp.stack(key_list[::-1])
    value_grads = jnp.stack(value_list[::-1])
    output_grads = jnp.stack(output_list[::-1])
    return (input_grads, query_grads, key_grads, value_grads, output_grads)
```

```python
import math

import jax
import jax.numpy as jnp
from jax import lax
from jax.sharding import PartitionSpec as P

HD = 128


epsilon = 1e-05
rope_base = 500000.0


def shifted(shard, axis, by):
    devices = lax.axis_size(axis)
    pairs = [(i, i + by) for i in range(devices) if 0 <= i + by < devices]
    return lax.ppermute(shard, axis, pairs)


def exchange_sum(blocks, axis):
    devices = lax.axis_size(axis)
    me = lax.axis_index(axis)
    total = lax.dynamic_index_in_dim(blocks, me, axis=0, keepdims=False).astype(jnp.float32)
    for by in range(1, devices):
        outgoing = lax.dynamic_index_in_dim(blocks, (me + by) % devices, axis=0, keepdims=False)
        incoming = lax.ppermute(outgoing, axis, [(i, (i + by) % devices) for i in range(devices)])
        total = total + incoming.astype(jnp.float32)
    return total


def position_tables(document_ids, head_dim):
    seq_len = document_ids.shape[1]
    index = jnp.arange(seq_len, dtype=jnp.int32)
    earlier = (document_ids[:, None, :] < document_ids[:, :, None]).astype(jnp.int32)
    position = index[None, :] - jnp.sum(earlier, axis=2)
    half = head_dim // 2
    expo = jnp.arange(half, dtype=jnp.float32) * (2.0 / head_dim)
    freq = jnp.exp(expo * -math.log(rope_base))
    angle = position.astype(jnp.float32)[:, :, None] * freq
    same = document_ids[:, :, None] == document_ids[:, None, :]
    causal = index[:, None] >= index[None, :]
    visible = jnp.logical_and(same, causal[None])
    return (jnp.cos(angle), jnp.sin(angle), visible)


def rotate(vector, rot_cos, rot_sin, direction):
    half = vector.shape[-1] // 2
    first = vector[..., :half]
    second = vector[..., half:]
    return jnp.concatenate(
        [
            first * rot_cos - direction * second * rot_sin,
            second * rot_cos + direction * first * rot_sin,
        ],
        axis=-1,
    )


def normalize(rows, gain):
    values = rows.astype(jnp.float32)
    inverse = lax.rsqrt(jnp.mean(values * values, axis=-1, keepdims=True) + epsilon)
    unit_rows = values * inverse
    normed = (unit_rows * gain.astype(jnp.float32)).astype(jnp.bfloat16)
    return (inverse, unit_rows, normed)


def attention_forward(query_rot, key_rot, value_low, visible):
    scale = 1.0 / math.sqrt(HD)
    scores = (
        jnp.einsum("bqngd,bknd->bngqk", query_rot, key_rot, preferred_element_type=jnp.float32)
        * scale
    )
    expo = jnp.where(visible[:, None, None], jnp.exp(scores), 0.0)
    prob = expo / jnp.sum(expo, axis=-1, keepdims=True)
    prob_low = prob.astype(jnp.bfloat16)
    mixed = jnp.einsum("bngqk,bknd->bqngd", prob_low, value_low, preferred_element_type=jnp.float32)
    return (prob, prob_low, mixed.astype(jnp.bfloat16))


def attention_backward(grad_mixed, query_rot, key_rot, value_low, prob, prob_low, rot_cos, rot_sin):
    scale = 1.0 / math.sqrt(HD)
    grad_value = jnp.einsum(
        "bngqk,bqngd->bknd", prob_low, grad_mixed, preferred_element_type=jnp.float32
    )
    grad_prob = jnp.einsum(
        "bqngd,bknd->bngqk", grad_mixed, value_low, preferred_element_type=jnp.float32
    )
    grad_score = prob * (grad_prob - jnp.sum(grad_prob * prob, axis=-1, keepdims=True)) * scale
    score_low = grad_score.astype(jnp.bfloat16)
    grad_query = jnp.einsum(
        "bngqk,bknd->bqngd", score_low, key_rot, preferred_element_type=jnp.float32
    )
    grad_key = jnp.einsum(
        "bngqk,bqngd->bknd", score_low, query_rot, preferred_element_type=jnp.float32
    )
    grad_query = rotate(
        grad_query, rot_cos[:, :, None, None, :], rot_sin[:, :, None, None, :], -1.0
    )
    grad_key = rotate(grad_key, rot_cos[:, :, None, :], rot_sin[:, :, None, :], -1.0)
    return (
        grad_query.astype(jnp.bfloat16),
        grad_key.astype(jnp.bfloat16),
        grad_value.astype(jnp.bfloat16),
    )


def back_norm(grad_normed, unit_rows, inverse, gain, incoming):
    grad_unit = grad_normed * gain.astype(jnp.float32)
    branch = (
        grad_unit - unit_rows * jnp.mean(grad_unit * unit_rows, axis=-1, keepdims=True)
    ) * inverse
    return (incoming.astype(jnp.float32) + branch).astype(jnp.bfloat16)


def local(
    section_inputs,
    norm_gain,
    query_weight,
    key_weight,
    value_weight,
    output_weight,
    upstream_grad,
    document_ids,
):
    pipes = lax.axis_size("pipe")
    section = lax.axis_index("pipe")
    groups = lax.axis_size("dp")
    width = section_inputs.shape[2]
    seq_len = document_ids.shape[1]
    q_width = query_weight.shape[2]
    k_width = key_weight.shape[2]
    kv_local = k_width // HD
    group = q_width // k_width
    gain = norm_gain[0]
    w_query = query_weight[0]
    w_key = key_weight[0]
    w_value = value_weight[0]
    w_output = output_weight[0]
    rot_cos, rot_sin, visible = position_tables(document_ids, HD)
    last = pipes - 1
    inverse, unit_rows, normed_shard = normalize(section_inputs[0], gain)
    normed = lax.all_gather(normed_shard, "tensor", axis=0, tiled=True)
    incoming = jnp.where(section == last, upstream_grad, jnp.zeros_like(upstream_grad))
    query = jnp.dot(normed, w_query, preferred_element_type=jnp.float32).reshape(
        1, seq_len, kv_local, group, HD
    )
    keys = jnp.dot(normed, w_key, preferred_element_type=jnp.float32).reshape(
        1, seq_len, kv_local, HD
    )
    values = jnp.dot(normed, w_value, preferred_element_type=jnp.float32).reshape(
        1, seq_len, kv_local, HD
    )
    query_rot = rotate(
        query, rot_cos[:, :, None, None, :], rot_sin[:, :, None, None, :], 1.0
    ).astype(jnp.bfloat16)
    key_rot = rotate(keys, rot_cos[:, :, None, :], rot_sin[:, :, None, :], 1.0).astype(jnp.bfloat16)
    value_low = values.astype(jnp.bfloat16)
    prob, prob_low, mixed = attention_forward(query_rot, key_rot, value_low, visible)
    mixed_flat = mixed.reshape(seq_len, q_width)

    def backward_turn(cotangent):
        grad_mixed = jnp.einsum(
            "sd,hd->sh", cotangent, w_output, preferred_element_type=jnp.float32
        )
        grad_mixed = grad_mixed.astype(jnp.bfloat16).reshape(1, seq_len, kv_local, group, HD)
        grad_query, grad_key, grad_value = attention_backward(
            grad_mixed, query_rot, key_rot, value_low, prob, prob_low, rot_cos, rot_sin
        )
        flat_query = grad_query.reshape(seq_len, q_width)
        flat_key = grad_key.reshape(seq_len, k_width)
        flat_value = grad_value.reshape(seq_len, k_width)
        grad_normed = (
            jnp.einsum("sh,dh->sd", flat_query, w_query, preferred_element_type=jnp.float32)
            + jnp.einsum("sh,dh->sd", flat_key, w_key, preferred_element_type=jnp.float32)
            + jnp.einsum("sh,dh->sd", flat_value, w_value, preferred_element_type=jnp.float32)
        )
        return (grad_normed.astype(jnp.bfloat16), flat_query, flat_key, flat_value)

    def skipped_turn(cotangent):
        return (
            jnp.zeros((seq_len, width), jnp.bfloat16),
            jnp.zeros((seq_len, q_width), jnp.bfloat16),
            jnp.zeros((seq_len, k_width), jnp.bfloat16),
            jnp.zeros((seq_len, k_width), jnp.bfloat16),
        )

    saved_query = jnp.zeros((seq_len, q_width), jnp.bfloat16)
    saved_key = jnp.zeros((seq_len, k_width), jnp.bfloat16)
    saved_value = jnp.zeros((seq_len, k_width), jnp.bfloat16)
    saved_cot = jnp.zeros((seq_len, width), jnp.bfloat16)
    saved_input = jnp.zeros_like(incoming)
    for turn in range(pipes):
        active = section == last - turn
        cotangent = lax.all_gather(incoming, "tensor", axis=0, tiled=True)
        grad_normed, flat_query, flat_key, flat_value = lax.cond(
            active, backward_turn, skipped_turn, cotangent
        )
        tensors = lax.axis_size("tensor")
        summed = exchange_sum(grad_normed.reshape(tensors, seq_len // tensors, width), "tensor")
        result = back_norm(summed, unit_rows, inverse, gain, incoming)
        saved_query = jnp.where(active, flat_query, saved_query)
        saved_key = jnp.where(active, flat_key, saved_key)
        saved_value = jnp.where(active, flat_value, saved_value)
        saved_cot = jnp.where(active, cotangent, saved_cot)
        saved_input = jnp.where(active, result, saved_input)
        if turn + 1 < pipes:
            incoming = shifted(result, "pipe", -1)
    scale_out = 1.0 / math.sqrt(groups * seq_len)
    grads_qkv = jnp.concatenate([saved_query, saved_key, saved_value], axis=1)
    terms = jnp.concatenate(
        [
            jnp.einsum("sd,sh->dh", normed, grads_qkv, preferred_element_type=jnp.float32).astype(
                jnp.bfloat16
            ),
            jnp.einsum("sd,sh->dh", saved_cot, mixed_flat, preferred_element_type=jnp.float32).astype(
                jnp.bfloat16
            ),
        ],
        axis=1,
    )
    sums = exchange_sum(terms.reshape(groups, width // groups, terms.shape[1]), "dp") * scale_out
    query_grads = sums[:, :q_width][None]
    key_grads = sums[:, q_width : q_width + k_width][None]
    value_grads = sums[:, q_width + k_width : q_width + 2 * k_width][None]
    output_grads = sums[:, q_width + 2 * k_width :].T[None]
    return (saved_input[None], query_grads, key_grads, value_grads, output_grads)


def solution(mesh):
    placed = (
        P("pipe", ("dp", "tensor"), None),
        P("pipe", None),
        P("pipe", None, "tensor"),
        P("pipe", None, "tensor"),
        P("pipe", None, "tensor"),
        P("pipe", "tensor", None),
        P(("dp", "tensor"), None),
        P("dp", None),
    )
    return jax.shard_map(
        local,
        mesh=mesh,
        in_specs=placed,
        out_specs=(
            P("pipe", ("dp", "tensor"), None),
            P("pipe", "dp", "tensor"),
            P("pipe", "dp", "tensor"),
            P("pipe", "dp", "tensor"),
            P("pipe", "tensor", "dp"),
        ),
        check_vma=False,
    )
```

```python
import math

import jax
import jax.numpy as jnp
from jax import lax
from jax.sharding import PartitionSpec as P

HD = 128


epsilon = 1e-05
rope_base = 500000.0


def shifted(shard, axis, by):
    devices = lax.axis_size(axis)
    pairs = [(i, i + by) for i in range(devices) if 0 <= i + by < devices]
    return lax.ppermute(shard, axis, pairs)


def exchange_sum(blocks, axis, dim=0):
    devices = lax.axis_size(axis)
    me = lax.axis_index(axis)
    total = lax.dynamic_index_in_dim(blocks, me, axis=dim, keepdims=False).astype(jnp.float32)
    for by in range(1, devices):
        outgoing = lax.dynamic_index_in_dim(blocks, (me + by) % devices, axis=dim, keepdims=False)
        incoming = lax.ppermute(outgoing, axis, [(i, (i + by) % devices) for i in range(devices)])
        total = total + incoming.astype(jnp.float32)
    return total


def position_tables(document_ids, head_dim):
    seq_len = document_ids.shape[1]
    index = jnp.arange(seq_len, dtype=jnp.int32)
    earlier = (document_ids[:, None, :] < document_ids[:, :, None]).astype(jnp.int32)
    position = index[None, :] - jnp.sum(earlier, axis=2)
    half = head_dim // 2
    expo = jnp.arange(half, dtype=jnp.float32) * (2.0 / head_dim)
    freq = jnp.exp(expo * -math.log(rope_base))
    angle = position.astype(jnp.float32)[:, :, None] * freq
    same = document_ids[:, :, None] == document_ids[:, None, :]
    causal = index[:, None] >= index[None, :]
    visible = jnp.logical_and(same, causal[None])
    return (jnp.cos(angle), jnp.sin(angle), visible)


def rotate(vector, rot_cos, rot_sin, direction):
    half = vector.shape[-1] // 2
    first = vector[..., :half]
    second = vector[..., half:]
    return jnp.concatenate(
        [
            first * rot_cos - direction * second * rot_sin,
            second * rot_cos + direction * first * rot_sin,
        ],
        axis=-1,
    )


def normalize(rows, gain):
    values = rows.astype(jnp.float32)
    inverse = lax.rsqrt(jnp.mean(values * values, axis=-1, keepdims=True) + epsilon)
    unit_rows = values * inverse
    normed = (unit_rows * gain.astype(jnp.float32)).astype(jnp.bfloat16)
    return (inverse, unit_rows, normed)


def attention_forward(query_rot, key_rot, value_low, visible):
    scale = 1.0 / math.sqrt(HD)
    scores = (
        jnp.einsum("bqngd,bknd->bngqk", query_rot, key_rot, preferred_element_type=jnp.float32)
        * scale
    )
    expo = jnp.where(visible[:, None, None], jnp.exp(scores), 0.0)
    prob = expo / jnp.sum(expo, axis=-1, keepdims=True)
    prob_low = prob.astype(jnp.bfloat16)
    mixed = jnp.einsum("bngqk,bknd->bqngd", prob_low, value_low, preferred_element_type=jnp.float32)
    return (prob, prob_low, mixed.astype(jnp.bfloat16))


def attention_backward(grad_mixed, query_rot, key_rot, value_low, prob, prob_low, rot_cos, rot_sin):
    scale = 1.0 / math.sqrt(HD)
    grad_value = jnp.einsum(
        "bngqk,bqngd->bknd", prob_low, grad_mixed, preferred_element_type=jnp.float32
    )
    grad_prob = jnp.einsum(
        "bqngd,bknd->bngqk", grad_mixed, value_low, preferred_element_type=jnp.float32
    )
    grad_score = prob * (grad_prob - jnp.sum(grad_prob * prob, axis=-1, keepdims=True)) * scale
    score_low = grad_score.astype(jnp.bfloat16)
    grad_query = jnp.einsum(
        "bngqk,bknd->bqngd", score_low, key_rot, preferred_element_type=jnp.float32
    )
    grad_key = jnp.einsum(
        "bngqk,bqngd->bknd", score_low, query_rot, preferred_element_type=jnp.float32
    )
    grad_query = rotate(
        grad_query, rot_cos[:, :, None, None, :], rot_sin[:, :, None, None, :], -1.0
    )
    grad_key = rotate(grad_key, rot_cos[:, :, None, :], rot_sin[:, :, None, :], -1.0)
    return (
        grad_query.astype(jnp.bfloat16),
        grad_key.astype(jnp.bfloat16),
        grad_value.astype(jnp.bfloat16),
    )


def back_norm(grad_normed, unit_rows, inverse, gain, incoming):
    grad_unit = grad_normed * gain.astype(jnp.float32)
    branch = (
        grad_unit - unit_rows * jnp.mean(grad_unit * unit_rows, axis=-1, keepdims=True)
    ) * inverse
    return (incoming.astype(jnp.float32) + branch).astype(jnp.bfloat16)


def local(
    section_inputs,
    norm_gain,
    query_weight,
    key_weight,
    value_weight,
    output_weight,
    upstream_grad,
    document_ids,
):
    pipes = lax.axis_size("pipe")
    section = lax.axis_index("pipe")
    groups = lax.axis_size("dp")
    width = section_inputs.shape[2]
    seq_len = document_ids.shape[1]
    q_width = query_weight.shape[2]
    k_width = key_weight.shape[2]
    kv_local = k_width // HD
    group = q_width // k_width
    gain = norm_gain[0]
    w_query = query_weight[0]
    w_key = key_weight[0]
    w_value = value_weight[0]
    w_output = output_weight[0]
    rot_cos, rot_sin, visible = position_tables(document_ids, HD)
    last = pipes - 1
    inverse, unit_rows, normed_shard = normalize(section_inputs[0], gain)
    normed = lax.all_gather(normed_shard, "tensor", axis=0, tiled=True)
    incoming = jnp.where(section == last, upstream_grad, jnp.zeros_like(upstream_grad))
    query = jnp.dot(normed, w_query, preferred_element_type=jnp.float32).reshape(
        1, seq_len, kv_local, group, HD
    )
    keys = jnp.dot(normed, w_key, preferred_element_type=jnp.float32).reshape(
        1, seq_len, kv_local, HD
    )
    values = jnp.dot(normed, w_value, preferred_element_type=jnp.float32).reshape(
        1, seq_len, kv_local, HD
    )
    query_rot = rotate(
        query, rot_cos[:, :, None, None, :], rot_sin[:, :, None, None, :], 1.0
    ).astype(jnp.bfloat16)
    key_rot = rotate(keys, rot_cos[:, :, None, :], rot_sin[:, :, None, :], 1.0).astype(jnp.bfloat16)
    value_low = values.astype(jnp.bfloat16)
    prob, prob_low, mixed = attention_forward(query_rot, key_rot, value_low, visible)
    mixed_flat = mixed.reshape(seq_len, q_width)

    def backward_turn(cotangent):
        grad_mixed = jnp.einsum(
            "sd,hd->sh", cotangent, w_output, preferred_element_type=jnp.float32
        )
        grad_mixed = grad_mixed.astype(jnp.bfloat16).reshape(1, seq_len, kv_local, group, HD)
        grad_query, grad_key, grad_value = attention_backward(
            grad_mixed, query_rot, key_rot, value_low, prob, prob_low, rot_cos, rot_sin
        )
        flat_query = grad_query.reshape(seq_len, q_width)
        flat_key = grad_key.reshape(seq_len, k_width)
        flat_value = grad_value.reshape(seq_len, k_width)
        grad_normed = (
            jnp.einsum("sh,dh->sd", flat_query, w_query, preferred_element_type=jnp.float32)
            + jnp.einsum("sh,dh->sd", flat_key, w_key, preferred_element_type=jnp.float32)
            + jnp.einsum("sh,dh->sd", flat_value, w_value, preferred_element_type=jnp.float32)
        )
        return (grad_normed.astype(jnp.bfloat16), flat_query, flat_key, flat_value)

    def skipped_turn(cotangent):
        return (
            jnp.zeros((seq_len, width), jnp.bfloat16),
            jnp.zeros((seq_len, q_width), jnp.bfloat16),
            jnp.zeros((seq_len, k_width), jnp.bfloat16),
            jnp.zeros((seq_len, k_width), jnp.bfloat16),
        )

    saved_query = jnp.zeros((seq_len, q_width), jnp.bfloat16)
    saved_key = jnp.zeros((seq_len, k_width), jnp.bfloat16)
    saved_value = jnp.zeros((seq_len, k_width), jnp.bfloat16)
    saved_cot = jnp.zeros((seq_len, width), jnp.bfloat16)
    saved_input = jnp.zeros_like(incoming)
    for turn in range(pipes):
        active = section == last - turn
        cotangent = lax.all_gather(incoming, "tensor", axis=0, tiled=True)
        grad_normed, flat_query, flat_key, flat_value = lax.cond(
            active, backward_turn, skipped_turn, cotangent
        )
        tensors = lax.axis_size("tensor")
        summed = exchange_sum(grad_normed.reshape(tensors, seq_len // tensors, width), "tensor")
        result = back_norm(summed, unit_rows, inverse, gain, incoming)
        saved_query = jnp.where(active, flat_query, saved_query)
        saved_key = jnp.where(active, flat_key, saved_key)
        saved_value = jnp.where(active, flat_value, saved_value)
        saved_cot = jnp.where(active, cotangent, saved_cot)
        saved_input = jnp.where(active, result, saved_input)
        if turn + 1 < pipes:
            incoming = shifted(result, "pipe", -1)
    scale_out = 1.0 / math.sqrt(groups * seq_len)
    block = width // groups
    out_term = jnp.einsum(
        "sh,sd->hd", mixed_flat, saved_cot, preferred_element_type=jnp.float32
    ).astype(jnp.bfloat16)
    output_grads = exchange_sum(out_term.reshape(q_width, groups, block), "dp", dim=1) * scale_out
    grads_qkv = jnp.concatenate([saved_query, saved_key, saved_value], axis=1)
    qkv_term = jnp.einsum(
        "sh,sd->hd", grads_qkv, normed, preferred_element_type=jnp.float32
    ).astype(jnp.bfloat16)
    sums = exchange_sum(qkv_term.reshape(qkv_term.shape[0], groups, block), "dp", dim=1).T * scale_out
    query_grads = sums[:, :q_width][None]
    key_grads = sums[:, q_width : q_width + k_width][None]
    value_grads = sums[:, q_width + k_width :][None]
    return (saved_input[None], query_grads, key_grads, value_grads, output_grads[None])


def solution(mesh):
    placed = (
        P("pipe", ("dp", "tensor"), None),
        P("pipe", None),
        P("pipe", None, "tensor"),
        P("pipe", None, "tensor"),
        P("pipe", None, "tensor"),
        P("pipe", "tensor", None),
        P(("dp", "tensor"), None),
        P("dp", None),
    )
    return jax.shard_map(
        local,
        mesh=mesh,
        in_specs=placed,
        out_specs=(
            P("pipe", ("dp", "tensor"), None),
            P("pipe", "dp", "tensor"),
            P("pipe", "dp", "tensor"),
            P("pipe", "dp", "tensor"),
            P("pipe", "tensor", "dp"),
        ),
        check_vma=False,
    )
```

```python
import math

import jax
import jax.numpy as jnp
from jax import lax
from jax.sharding import PartitionSpec as P

HD = 128


epsilon = 1e-05
rope_base = 500000.0


def shifted(shard, axis, by):
    devices = lax.axis_size(axis)
    pairs = [(i, i + by) for i in range(devices) if 0 <= i + by < devices]
    return lax.ppermute(shard, axis, pairs)


def exchange_sum(blocks, axis, dim=0):
    devices = lax.axis_size(axis)
    me = lax.axis_index(axis)
    total = lax.dynamic_index_in_dim(blocks, me, axis=dim, keepdims=False).astype(jnp.float32)
    for by in range(1, devices):
        outgoing = lax.dynamic_index_in_dim(blocks, (me + by) % devices, axis=dim, keepdims=False)
        incoming = lax.ppermute(outgoing, axis, [(i, (i + by) % devices) for i in range(devices)])
        total = total + incoming.astype(jnp.float32)
    return total


def position_tables(document_ids, head_dim):
    seq_len = document_ids.shape[1]
    index = jnp.arange(seq_len, dtype=jnp.int32)
    earlier = (document_ids[:, None, :] < document_ids[:, :, None]).astype(jnp.int32)
    position = index[None, :] - jnp.sum(earlier, axis=2)
    half = head_dim // 2
    expo = jnp.arange(half, dtype=jnp.float32) * (2.0 / head_dim)
    freq = jnp.exp(expo * -math.log(rope_base))
    angle = position.astype(jnp.float32)[:, :, None] * freq
    same = document_ids[:, :, None] == document_ids[:, None, :]
    causal = index[:, None] >= index[None, :]
    visible = jnp.logical_and(same, causal[None])
    return (jnp.cos(angle), jnp.sin(angle), visible)


def rotate(vector, rot_cos, rot_sin, direction):
    half = vector.shape[-1] // 2
    first = vector[..., :half]
    second = vector[..., half:]
    return jnp.concatenate(
        [
            first * rot_cos - direction * second * rot_sin,
            second * rot_cos + direction * first * rot_sin,
        ],
        axis=-1,
    )


def normalize(rows, gain):
    values = rows.astype(jnp.float32)
    inverse = lax.rsqrt(jnp.mean(values * values, axis=-1, keepdims=True) + epsilon)
    unit_rows = values * inverse
    normed = (unit_rows * gain.astype(jnp.float32)).astype(jnp.bfloat16)
    return (inverse, unit_rows, normed)


def attention_forward(query_rot, key_rot, value_low, visible):
    scale = 1.0 / math.sqrt(HD)
    scores = (
        jnp.einsum("bqngd,bknd->bngqk", query_rot, key_rot, preferred_element_type=jnp.float32)
        * scale
    )
    expo = jnp.where(visible[:, None, None], jnp.exp(scores), 0.0)
    prob = expo / jnp.sum(expo, axis=-1, keepdims=True)
    prob_low = prob.astype(jnp.bfloat16)
    mixed = jnp.einsum("bngqk,bknd->bqngd", prob_low, value_low, preferred_element_type=jnp.float32)
    return (prob, prob_low, mixed.astype(jnp.bfloat16))


def attention_backward(grad_mixed, query_rot, key_rot, value_low, prob, prob_low, rot_cos, rot_sin):
    scale = 1.0 / math.sqrt(HD)
    grad_value = jnp.einsum(
        "bngqk,bqngd->bknd", prob_low, grad_mixed, preferred_element_type=jnp.float32
    )
    grad_prob = jnp.einsum(
        "bqngd,bknd->bngqk", grad_mixed, value_low, preferred_element_type=jnp.float32
    )
    grad_score = prob * (grad_prob - jnp.sum(grad_prob * prob, axis=-1, keepdims=True)) * scale
    score_low = grad_score.astype(jnp.bfloat16)
    grad_query = jnp.einsum(
        "bngqk,bknd->bqngd", score_low, key_rot, preferred_element_type=jnp.float32
    )
    grad_key = jnp.einsum(
        "bngqk,bqngd->bknd", score_low, query_rot, preferred_element_type=jnp.float32
    )
    grad_query = rotate(
        grad_query, rot_cos[:, :, None, None, :], rot_sin[:, :, None, None, :], -1.0
    )
    grad_key = rotate(grad_key, rot_cos[:, :, None, :], rot_sin[:, :, None, :], -1.0)
    return (
        grad_query.astype(jnp.bfloat16),
        grad_key.astype(jnp.bfloat16),
        grad_value.astype(jnp.bfloat16),
    )


def back_norm(grad_normed, unit_rows, inverse, gain, incoming):
    grad_unit = grad_normed * gain.astype(jnp.float32)
    branch = (
        grad_unit - unit_rows * jnp.mean(grad_unit * unit_rows, axis=-1, keepdims=True)
    ) * inverse
    return (incoming.astype(jnp.float32) + branch).astype(jnp.bfloat16)


def local(
    section_inputs,
    norm_gain,
    query_weight,
    key_weight,
    value_weight,
    output_weight,
    upstream_grad,
    document_ids,
):
    pipes = lax.axis_size("pipe")
    section = lax.axis_index("pipe")
    groups = lax.axis_size("dp")
    width = section_inputs.shape[2]
    seq_len = document_ids.shape[1]
    q_width = query_weight.shape[2]
    k_width = key_weight.shape[2]
    kv_local = k_width // HD
    group = q_width // k_width
    gain = norm_gain[0]
    w_query = query_weight[0]
    w_key = key_weight[0]
    w_value = value_weight[0]
    w_output = output_weight[0]
    rot_cos, rot_sin, visible = position_tables(document_ids, HD)
    last = pipes - 1
    inverse, unit_rows, normed_shard = normalize(section_inputs[0], gain)
    normed = lax.all_gather(normed_shard, "tensor", axis=0, tiled=True)
    incoming = jnp.where(section == last, upstream_grad, jnp.zeros_like(upstream_grad))
    query = jnp.dot(normed, w_query, preferred_element_type=jnp.float32).reshape(
        1, seq_len, kv_local, group, HD
    )
    keys = jnp.dot(normed, w_key, preferred_element_type=jnp.float32).reshape(
        1, seq_len, kv_local, HD
    )
    values = jnp.dot(normed, w_value, preferred_element_type=jnp.float32).reshape(
        1, seq_len, kv_local, HD
    )
    query_rot = rotate(
        query, rot_cos[:, :, None, None, :], rot_sin[:, :, None, None, :], 1.0
    ).astype(jnp.bfloat16)
    key_rot = rotate(keys, rot_cos[:, :, None, :], rot_sin[:, :, None, :], 1.0).astype(jnp.bfloat16)
    value_low = values.astype(jnp.bfloat16)
    prob, prob_low, mixed = attention_forward(query_rot, key_rot, value_low, visible)
    mixed_flat = mixed.reshape(seq_len, q_width)

    def backward_turn(cotangent):
        grad_mixed = jnp.einsum(
            "sd,hd->sh", cotangent, w_output, preferred_element_type=jnp.float32
        )
        grad_mixed = grad_mixed.astype(jnp.bfloat16).reshape(1, seq_len, kv_local, group, HD)
        grad_query, grad_key, grad_value = attention_backward(
            grad_mixed, query_rot, key_rot, value_low, prob, prob_low, rot_cos, rot_sin
        )
        flat_query = grad_query.reshape(seq_len, q_width)
        flat_key = grad_key.reshape(seq_len, k_width)
        flat_value = grad_value.reshape(seq_len, k_width)
        grad_normed = (
            jnp.einsum("sh,dh->sd", flat_query, w_query, preferred_element_type=jnp.float32)
            + jnp.einsum("sh,dh->sd", flat_key, w_key, preferred_element_type=jnp.float32)
            + jnp.einsum("sh,dh->sd", flat_value, w_value, preferred_element_type=jnp.float32)
        )
        return (grad_normed.astype(jnp.bfloat16), flat_query, flat_key, flat_value)

    def skipped_turn(cotangent):
        return (
            jnp.zeros((seq_len, width), jnp.bfloat16),
            jnp.zeros((seq_len, q_width), jnp.bfloat16),
            jnp.zeros((seq_len, k_width), jnp.bfloat16),
            jnp.zeros((seq_len, k_width), jnp.bfloat16),
        )

    saved_query = jnp.zeros((seq_len, q_width), jnp.bfloat16)
    saved_key = jnp.zeros((seq_len, k_width), jnp.bfloat16)
    saved_value = jnp.zeros((seq_len, k_width), jnp.bfloat16)
    saved_cot = jnp.zeros((seq_len, width), jnp.bfloat16)
    saved_input = jnp.zeros_like(incoming)
    for turn in range(pipes):
        active = section == last - turn
        cotangent = lax.all_gather(incoming, "tensor", axis=0, tiled=True)
        grad_normed, flat_query, flat_key, flat_value = lax.cond(
            active, backward_turn, skipped_turn, cotangent
        )
        tensors = lax.axis_size("tensor")
        summed = exchange_sum(grad_normed.reshape(tensors, seq_len // tensors, width), "tensor")
        result = back_norm(summed, unit_rows, inverse, gain, incoming)
        saved_query = jnp.where(active, flat_query, saved_query)
        saved_key = jnp.where(active, flat_key, saved_key)
        saved_value = jnp.where(active, flat_value, saved_value)
        saved_cot = jnp.where(active, cotangent, saved_cot)
        saved_input = jnp.where(active, result, saved_input)
        if turn + 1 < pipes:
            incoming = shifted(result, "pipe", -1)
    scale_out = 1.0 / math.sqrt(groups * seq_len)
    block = width // groups
    out_term = jnp.einsum(
        "sh,sjd->jhd",
        mixed_flat,
        saved_cot.reshape(seq_len, groups, block),
        preferred_element_type=jnp.float32,
    ).astype(jnp.bfloat16)
    out_parts = lax.all_to_all(out_term, "dp", 0, 0, tiled=True)
    output_grads = jnp.sum(out_parts.astype(jnp.float32), axis=0) * scale_out
    grads_qkv = jnp.concatenate([saved_query, saved_key, saved_value], axis=1)
    qkv_term = jnp.einsum(
        "sh,sjd->jhd",
        grads_qkv,
        normed.reshape(seq_len, groups, block),
        preferred_element_type=jnp.float32,
    ).astype(jnp.bfloat16)
    qkv_parts = lax.all_to_all(qkv_term, "dp", 0, 0, tiled=True)
    sums = jnp.sum(qkv_parts.astype(jnp.float32), axis=0).T * scale_out
    query_grads = sums[:, :q_width][None]
    key_grads = sums[:, q_width : q_width + k_width][None]
    value_grads = sums[:, q_width + k_width :][None]
    return (saved_input[None], query_grads, key_grads, value_grads, output_grads[None])


def solution(mesh):
    placed = (
        P("pipe", ("dp", "tensor"), None),
        P("pipe", None),
        P("pipe", None, "tensor"),
        P("pipe", None, "tensor"),
        P("pipe", None, "tensor"),
        P("pipe", "tensor", None),
        P(("dp", "tensor"), None),
        P("dp", None),
    )
    return jax.shard_map(
        local,
        mesh=mesh,
        in_specs=placed,
        out_specs=(
            P("pipe", ("dp", "tensor"), None),
            P("pipe", "dp", "tensor"),
            P("pipe", "dp", "tensor"),
            P("pipe", "dp", "tensor"),
            P("pipe", "tensor", "dp"),
        ),
        check_vma=False,
    )
```

```python
import math

import jax
import jax.numpy as jnp
from jax import lax
from jax.sharding import PartitionSpec as P

HD = 128


epsilon = 1e-05
rope_base = 500000.0


def shifted(shard, axis, by):
    devices = lax.axis_size(axis)
    pairs = [(i, i + by) for i in range(devices) if 0 <= i + by < devices]
    return lax.ppermute(shard, axis, pairs)


def exchange_sum(blocks, axis, dim=0):
    devices = lax.axis_size(axis)
    me = lax.axis_index(axis)
    total = lax.dynamic_index_in_dim(blocks, me, axis=dim, keepdims=False).astype(jnp.float32)
    for by in range(1, devices):
        outgoing = lax.dynamic_index_in_dim(blocks, (me + by) % devices, axis=dim, keepdims=False)
        incoming = lax.ppermute(outgoing, axis, [(i, (i + by) % devices) for i in range(devices)])
        total = total + incoming.astype(jnp.float32)
    return total


def position_tables(document_ids, head_dim):
    seq_len = document_ids.shape[1]
    index = jnp.arange(seq_len, dtype=jnp.int32)
    earlier = (document_ids[:, None, :] < document_ids[:, :, None]).astype(jnp.int32)
    position = index[None, :] - jnp.sum(earlier, axis=2)
    half = head_dim // 2
    expo = jnp.arange(half, dtype=jnp.float32) * (2.0 / head_dim)
    freq = jnp.exp(expo * -math.log(rope_base))
    angle = position.astype(jnp.float32)[:, :, None] * freq
    same = document_ids[:, :, None] == document_ids[:, None, :]
    causal = index[:, None] >= index[None, :]
    visible = jnp.logical_and(same, causal[None])
    return (jnp.cos(angle), jnp.sin(angle), visible)


def rotate(vector, rot_cos, rot_sin, direction):
    half = vector.shape[-1] // 2
    first = vector[..., :half]
    second = vector[..., half:]
    return jnp.concatenate(
        [
            first * rot_cos - direction * second * rot_sin,
            second * rot_cos + direction * first * rot_sin,
        ],
        axis=-1,
    )


def normalize(rows, gain):
    values = rows.astype(jnp.float32)
    inverse = lax.rsqrt(jnp.mean(values * values, axis=-1, keepdims=True) + epsilon)
    unit_rows = values * inverse
    normed = (unit_rows * gain.astype(jnp.float32)).astype(jnp.bfloat16)
    return (inverse, unit_rows, normed)


def attention_forward(query_rot, key_rot, value_low, visible):
    scale = 1.0 / math.sqrt(HD)
    scores = (
        jnp.einsum("bqngd,bknd->bngqk", query_rot, key_rot, preferred_element_type=jnp.float32)
        * scale
    )
    expo = jnp.where(visible[:, None, None], jnp.exp(scores), 0.0)
    prob = expo / jnp.sum(expo, axis=-1, keepdims=True)
    prob_low = prob.astype(jnp.bfloat16)
    mixed = jnp.einsum("bngqk,bknd->bqngd", prob_low, value_low, preferred_element_type=jnp.float32)
    return (prob, prob_low, mixed.astype(jnp.bfloat16))


def attention_backward(grad_mixed, query_rot, key_rot, value_low, prob, prob_low, rot_cos, rot_sin):
    scale = 1.0 / math.sqrt(HD)
    grad_value = jnp.einsum(
        "bngqk,bqngd->bknd", prob_low, grad_mixed, preferred_element_type=jnp.float32
    )
    grad_prob = jnp.einsum(
        "bqngd,bknd->bngqk", grad_mixed, value_low, preferred_element_type=jnp.float32
    )
    grad_score = prob * (grad_prob - jnp.sum(grad_prob * prob, axis=-1, keepdims=True)) * scale
    score_low = grad_score.astype(jnp.bfloat16)
    grad_query = jnp.einsum(
        "bngqk,bknd->bqngd", score_low, key_rot, preferred_element_type=jnp.float32
    )
    grad_key = jnp.einsum(
        "bngqk,bqngd->bknd", score_low, query_rot, preferred_element_type=jnp.float32
    )
    grad_query = rotate(
        grad_query, rot_cos[:, :, None, None, :], rot_sin[:, :, None, None, :], -1.0
    )
    grad_key = rotate(grad_key, rot_cos[:, :, None, :], rot_sin[:, :, None, :], -1.0)
    return (
        grad_query.astype(jnp.bfloat16),
        grad_key.astype(jnp.bfloat16),
        grad_value.astype(jnp.bfloat16),
    )


def back_norm(grad_normed, unit_rows, inverse, gain, incoming):
    grad_unit = grad_normed * gain.astype(jnp.float32)
    branch = (
        grad_unit - unit_rows * jnp.mean(grad_unit * unit_rows, axis=-1, keepdims=True)
    ) * inverse
    return (incoming.astype(jnp.float32) + branch).astype(jnp.bfloat16)


def local(
    section_inputs,
    norm_gain,
    query_weight,
    key_weight,
    value_weight,
    output_weight,
    upstream_grad,
    document_ids,
):
    pipes = lax.axis_size("pipe")
    section = lax.axis_index("pipe")
    groups = lax.axis_size("dp")
    width = section_inputs.shape[2]
    seq_len = document_ids.shape[1]
    q_width = query_weight.shape[2]
    k_width = key_weight.shape[2]
    kv_local = k_width // HD
    group = q_width // k_width
    gain = norm_gain[0]
    w_query = query_weight[0]
    w_key = key_weight[0]
    w_value = value_weight[0]
    w_output = output_weight[0]
    rot_cos, rot_sin, visible = position_tables(document_ids, HD)
    last = pipes - 1
    inverse, unit_rows, normed_shard = normalize(section_inputs[0], gain)
    normed = lax.all_gather(normed_shard, "tensor", axis=0, tiled=True)
    incoming = jnp.where(section == last, upstream_grad, jnp.zeros_like(upstream_grad))
    query = jnp.dot(normed, w_query, preferred_element_type=jnp.float32).reshape(
        1, seq_len, kv_local, group, HD
    )
    keys = jnp.dot(normed, w_key, preferred_element_type=jnp.float32).reshape(
        1, seq_len, kv_local, HD
    )
    values = jnp.dot(normed, w_value, preferred_element_type=jnp.float32).reshape(
        1, seq_len, kv_local, HD
    )
    query_rot = rotate(
        query, rot_cos[:, :, None, None, :], rot_sin[:, :, None, None, :], 1.0
    ).astype(jnp.bfloat16)
    key_rot = rotate(keys, rot_cos[:, :, None, :], rot_sin[:, :, None, :], 1.0).astype(jnp.bfloat16)
    value_low = values.astype(jnp.bfloat16)
    prob, prob_low, mixed = attention_forward(query_rot, key_rot, value_low, visible)
    mixed_flat = mixed.reshape(seq_len, q_width)

    def backward_turn(cotangent):
        grad_mixed = jnp.einsum(
            "sd,hd->sh", cotangent, w_output, preferred_element_type=jnp.float32
        )
        grad_mixed = grad_mixed.astype(jnp.bfloat16).reshape(1, seq_len, kv_local, group, HD)
        grad_query, grad_key, grad_value = attention_backward(
            grad_mixed, query_rot, key_rot, value_low, prob, prob_low, rot_cos, rot_sin
        )
        flat_query = grad_query.reshape(seq_len, q_width)
        flat_key = grad_key.reshape(seq_len, k_width)
        flat_value = grad_value.reshape(seq_len, k_width)
        grad_normed = (
            jnp.einsum("sh,dh->sd", flat_query, w_query, preferred_element_type=jnp.float32)
            + jnp.einsum("sh,dh->sd", flat_key, w_key, preferred_element_type=jnp.float32)
            + jnp.einsum("sh,dh->sd", flat_value, w_value, preferred_element_type=jnp.float32)
        )
        return (grad_normed.astype(jnp.bfloat16), flat_query, flat_key, flat_value)

    def skipped_turn(cotangent):
        return (
            jnp.zeros((seq_len, width), jnp.bfloat16),
            jnp.zeros((seq_len, q_width), jnp.bfloat16),
            jnp.zeros((seq_len, k_width), jnp.bfloat16),
            jnp.zeros((seq_len, k_width), jnp.bfloat16),
        )

    saved_query = jnp.zeros((seq_len, q_width), jnp.bfloat16)
    saved_key = jnp.zeros((seq_len, k_width), jnp.bfloat16)
    saved_value = jnp.zeros((seq_len, k_width), jnp.bfloat16)
    saved_cot = jnp.zeros((seq_len, width), jnp.bfloat16)
    saved_input = jnp.zeros_like(incoming)
    tensors = lax.axis_size("tensor")
    rows = seq_len // tensors
    halves = 2
    half = rows // halves
    parts = [incoming[h * half : (h + 1) * half] for h in range(halves)]
    for turn in range(pipes):
        active = section == last - turn
        gathered = [lax.all_gather(part, "tensor", axis=0, tiled=True) for part in parts]
        cotangent = jnp.stack(
            [piece.reshape(tensors, half, width) for piece in gathered], axis=1
        ).reshape(seq_len, width)
        grad_normed, flat_query, flat_key, flat_value = lax.cond(
            active, backward_turn, skipped_turn, cotangent
        )
        grad_blocks = grad_normed.reshape(tensors, halves, half, width)
        results = []
        for h in range(halves):
            rows_h = slice(h * half, (h + 1) * half)
            summed = exchange_sum(grad_blocks[:, h], "tensor")
            results.append(
                back_norm(summed, unit_rows[rows_h], inverse[rows_h], gain, parts[h])
            )
        result = jnp.concatenate(results, axis=0)
        saved_query = jnp.where(active, flat_query, saved_query)
        saved_key = jnp.where(active, flat_key, saved_key)
        saved_value = jnp.where(active, flat_value, saved_value)
        saved_cot = jnp.where(active, cotangent, saved_cot)
        saved_input = jnp.where(active, result, saved_input)
        if turn + 1 < pipes:
            pair = [(last - turn, last - turn - 1)]
            parts = [lax.ppermute(piece, "pipe", pair) for piece in results]
    scale_out = 1.0 / math.sqrt(groups * seq_len)
    block = width // groups
    out_term = jnp.einsum(
        "sh,sjd->jhd",
        mixed_flat,
        saved_cot.reshape(seq_len, groups, block),
        preferred_element_type=jnp.float32,
    ).astype(jnp.bfloat16)
    out_parts = lax.all_to_all(out_term, "dp", 0, 0, tiled=True)
    output_grads = jnp.sum(out_parts.astype(jnp.float32), axis=0) * scale_out
    grads_qkv = jnp.concatenate([saved_query, saved_key, saved_value], axis=1)
    qkv_term = jnp.einsum(
        "sh,sjd->jhd",
        grads_qkv,
        normed.reshape(seq_len, groups, block),
        preferred_element_type=jnp.float32,
    ).astype(jnp.bfloat16)
    qkv_parts = lax.all_to_all(qkv_term, "dp", 0, 0, tiled=True)
    sums = jnp.sum(qkv_parts.astype(jnp.float32), axis=0).T * scale_out
    query_grads = sums[:, :q_width][None]
    key_grads = sums[:, q_width : q_width + k_width][None]
    value_grads = sums[:, q_width + k_width :][None]
    return (saved_input[None], query_grads, key_grads, value_grads, output_grads[None])


def solution(mesh):
    placed = (
        P("pipe", ("dp", "tensor"), None),
        P("pipe", None),
        P("pipe", None, "tensor"),
        P("pipe", None, "tensor"),
        P("pipe", None, "tensor"),
        P("pipe", "tensor", None),
        P(("dp", "tensor"), None),
        P("dp", None),
    )
    return jax.shard_map(
        local,
        mesh=mesh,
        in_specs=placed,
        out_specs=(
            P("pipe", ("dp", "tensor"), None),
            P("pipe", "dp", "tensor"),
            P("pipe", "dp", "tensor"),
            P("pipe", "dp", "tensor"),
            P("pipe", "tensor", "dp"),
        ),
        check_vma=False,
    )
```

```python
import math

import jax
import jax.numpy as jnp
from jax import lax
from jax.sharding import PartitionSpec as P

HD = 128


epsilon = 1e-05
rope_base = 500000.0


def shifted(shard, axis, by):
    devices = lax.axis_size(axis)
    pairs = [(i, i + by) for i in range(devices) if 0 <= i + by < devices]
    return lax.ppermute(shard, axis, pairs)


def exchange_sum(blocks, axis, dim=0):
    devices = lax.axis_size(axis)
    me = lax.axis_index(axis)
    total = lax.dynamic_index_in_dim(blocks, me, axis=dim, keepdims=False).astype(jnp.float32)
    for by in range(1, devices):
        outgoing = lax.dynamic_index_in_dim(blocks, (me + by) % devices, axis=dim, keepdims=False)
        incoming = lax.ppermute(outgoing, axis, [(i, (i + by) % devices) for i in range(devices)])
        total = total + incoming.astype(jnp.float32)
    return total


def chip_pair_exchange_sum(blocks, axis):
    me = lax.axis_index(axis)
    pick = lambda index: lax.dynamic_index_in_dim(blocks, index, axis=0, keepdims=False)
    send = jnp.stack([pick(me ^ 1), pick(me ^ 3)])
    got = lax.ppermute(send, axis, [(i, i ^ 1) for i in range(4)])
    own = pick(me).astype(jnp.float32) + got[0].astype(jnp.float32)
    pair = pick(me ^ 2).astype(jnp.float32) + got[1].astype(jnp.float32)
    back = lax.ppermute(pair.astype(jnp.bfloat16), axis, [(i, i ^ 2) for i in range(4)])
    return own + back.astype(jnp.float32)


def position_tables(document_ids, head_dim):
    seq_len = document_ids.shape[1]
    index = jnp.arange(seq_len, dtype=jnp.int32)
    earlier = (document_ids[:, None, :] < document_ids[:, :, None]).astype(jnp.int32)
    position = index[None, :] - jnp.sum(earlier, axis=2)
    half = head_dim // 2
    expo = jnp.arange(half, dtype=jnp.float32) * (2.0 / head_dim)
    freq = jnp.exp(expo * -math.log(rope_base))
    angle = position.astype(jnp.float32)[:, :, None] * freq
    same = document_ids[:, :, None] == document_ids[:, None, :]
    causal = index[:, None] >= index[None, :]
    visible = jnp.logical_and(same, causal[None])
    return (jnp.cos(angle), jnp.sin(angle), visible)


def rotate(vector, rot_cos, rot_sin, direction):
    half = vector.shape[-1] // 2
    first = vector[..., :half]
    second = vector[..., half:]
    return jnp.concatenate(
        [
            first * rot_cos - direction * second * rot_sin,
            second * rot_cos + direction * first * rot_sin,
        ],
        axis=-1,
    )


def normalize(rows, gain):
    values = rows.astype(jnp.float32)
    inverse = lax.rsqrt(jnp.mean(values * values, axis=-1, keepdims=True) + epsilon)
    unit_rows = values * inverse
    normed = (unit_rows * gain.astype(jnp.float32)).astype(jnp.bfloat16)
    return (inverse, unit_rows, normed)


def attention_forward(query_rot, key_rot, value_low, visible):
    scale = 1.0 / math.sqrt(HD)
    scores = (
        jnp.einsum("bqngd,bknd->bngqk", query_rot, key_rot, preferred_element_type=jnp.float32)
        * scale
    )
    expo = jnp.where(visible[:, None, None], jnp.exp(scores), 0.0)
    prob = expo / jnp.sum(expo, axis=-1, keepdims=True)
    prob_low = prob.astype(jnp.bfloat16)
    mixed = jnp.einsum("bngqk,bknd->bqngd", prob_low, value_low, preferred_element_type=jnp.float32)
    return (prob, prob_low, mixed.astype(jnp.bfloat16))


def attention_backward(grad_mixed, query_rot, key_rot, value_low, prob, prob_low, rot_cos, rot_sin):
    scale = 1.0 / math.sqrt(HD)
    grad_value = jnp.einsum(
        "bngqk,bqngd->bknd", prob_low, grad_mixed, preferred_element_type=jnp.float32
    )
    grad_prob = jnp.einsum(
        "bqngd,bknd->bngqk", grad_mixed, value_low, preferred_element_type=jnp.float32
    )
    grad_score = prob * (grad_prob - jnp.sum(grad_prob * prob, axis=-1, keepdims=True)) * scale
    score_low = grad_score.astype(jnp.bfloat16)
    grad_query = jnp.einsum(
        "bngqk,bknd->bqngd", score_low, key_rot, preferred_element_type=jnp.float32
    )
    grad_key = jnp.einsum(
        "bngqk,bqngd->bknd", score_low, query_rot, preferred_element_type=jnp.float32
    )
    grad_query = rotate(
        grad_query, rot_cos[:, :, None, None, :], rot_sin[:, :, None, None, :], -1.0
    )
    grad_key = rotate(grad_key, rot_cos[:, :, None, :], rot_sin[:, :, None, :], -1.0)
    return (
        grad_query.astype(jnp.bfloat16),
        grad_key.astype(jnp.bfloat16),
        grad_value.astype(jnp.bfloat16),
    )


def back_norm(grad_normed, unit_rows, inverse, gain, incoming):
    grad_unit = grad_normed * gain.astype(jnp.float32)
    branch = (
        grad_unit - unit_rows * jnp.mean(grad_unit * unit_rows, axis=-1, keepdims=True)
    ) * inverse
    return (incoming.astype(jnp.float32) + branch).astype(jnp.bfloat16)


def local(
    section_inputs,
    norm_gain,
    query_weight,
    key_weight,
    value_weight,
    output_weight,
    upstream_grad,
    document_ids,
):
    pipes = lax.axis_size("pipe")
    section = lax.axis_index("pipe")
    groups = lax.axis_size("dp")
    width = section_inputs.shape[2]
    seq_len = document_ids.shape[1]
    q_width = query_weight.shape[2]
    k_width = key_weight.shape[2]
    kv_local = k_width // HD
    group = q_width // k_width
    gain = norm_gain[0]
    w_query = query_weight[0]
    w_key = key_weight[0]
    w_value = value_weight[0]
    w_output = output_weight[0]
    rot_cos, rot_sin, visible = position_tables(document_ids, HD)
    last = pipes - 1
    inverse, unit_rows, normed_shard = normalize(section_inputs[0], gain)
    normed = lax.all_gather(normed_shard, "tensor", axis=0, tiled=True)
    incoming = jnp.where(section == last, upstream_grad, jnp.zeros_like(upstream_grad))
    query = jnp.dot(normed, w_query, preferred_element_type=jnp.float32).reshape(
        1, seq_len, kv_local, group, HD
    )
    keys = jnp.dot(normed, w_key, preferred_element_type=jnp.float32).reshape(
        1, seq_len, kv_local, HD
    )
    values = jnp.dot(normed, w_value, preferred_element_type=jnp.float32).reshape(
        1, seq_len, kv_local, HD
    )
    query_rot = rotate(
        query, rot_cos[:, :, None, None, :], rot_sin[:, :, None, None, :], 1.0
    ).astype(jnp.bfloat16)
    key_rot = rotate(keys, rot_cos[:, :, None, :], rot_sin[:, :, None, :], 1.0).astype(jnp.bfloat16)
    value_low = values.astype(jnp.bfloat16)
    prob, prob_low, mixed = attention_forward(query_rot, key_rot, value_low, visible)
    mixed_flat = mixed.reshape(seq_len, q_width)

    def backward_turn(cotangent):
        grad_mixed = jnp.einsum(
            "sd,hd->sh", cotangent, w_output, preferred_element_type=jnp.float32
        )
        grad_mixed = grad_mixed.astype(jnp.bfloat16).reshape(1, seq_len, kv_local, group, HD)
        grad_query, grad_key, grad_value = attention_backward(
            grad_mixed, query_rot, key_rot, value_low, prob, prob_low, rot_cos, rot_sin
        )
        flat_query = grad_query.reshape(seq_len, q_width)
        flat_key = grad_key.reshape(seq_len, k_width)
        flat_value = grad_value.reshape(seq_len, k_width)
        grad_normed = (
            jnp.einsum("sh,dh->sd", flat_query, w_query, preferred_element_type=jnp.float32)
            + jnp.einsum("sh,dh->sd", flat_key, w_key, preferred_element_type=jnp.float32)
            + jnp.einsum("sh,dh->sd", flat_value, w_value, preferred_element_type=jnp.float32)
        )
        return (grad_normed.astype(jnp.bfloat16), flat_query, flat_key, flat_value)

    def skipped_turn(cotangent):
        return (
            jnp.zeros((seq_len, width), jnp.bfloat16),
            jnp.zeros((seq_len, q_width), jnp.bfloat16),
            jnp.zeros((seq_len, k_width), jnp.bfloat16),
            jnp.zeros((seq_len, k_width), jnp.bfloat16),
        )

    saved_query = jnp.zeros((seq_len, q_width), jnp.bfloat16)
    saved_key = jnp.zeros((seq_len, k_width), jnp.bfloat16)
    saved_value = jnp.zeros((seq_len, k_width), jnp.bfloat16)
    saved_cot = jnp.zeros((seq_len, width), jnp.bfloat16)
    saved_input = jnp.zeros_like(incoming)
    for turn in range(pipes):
        active = section == last - turn
        cotangent = lax.all_gather(incoming, "tensor", axis=0, tiled=True)
        grad_normed, flat_query, flat_key, flat_value = lax.cond(
            active, backward_turn, skipped_turn, cotangent
        )
        tensors = lax.axis_size("tensor")
        grad_blocks = grad_normed.reshape(tensors, seq_len // tensors, width)
        if tensors == 4:
            summed = chip_pair_exchange_sum(grad_blocks, "tensor")
        else:
            summed = exchange_sum(grad_blocks, "tensor")
        result = back_norm(summed, unit_rows, inverse, gain, incoming)
        saved_query = jnp.where(active, flat_query, saved_query)
        saved_key = jnp.where(active, flat_key, saved_key)
        saved_value = jnp.where(active, flat_value, saved_value)
        saved_cot = jnp.where(active, cotangent, saved_cot)
        saved_input = jnp.where(active, result, saved_input)
        if turn + 1 < pipes:
            incoming = shifted(result, "pipe", -1)
    scale_out = 1.0 / math.sqrt(groups * seq_len)
    block = width // groups
    out_term = jnp.einsum(
        "sh,sjd->jhd",
        mixed_flat,
        saved_cot.reshape(seq_len, groups, block),
        preferred_element_type=jnp.float32,
    ).astype(jnp.bfloat16)
    out_parts = lax.all_to_all(out_term, "dp", 0, 0, tiled=True)
    output_grads = jnp.sum(out_parts.astype(jnp.float32), axis=0) * scale_out
    grads_qkv = jnp.concatenate([saved_query, saved_key, saved_value], axis=1)
    qkv_term = jnp.einsum(
        "sh,sjd->jhd",
        grads_qkv,
        normed.reshape(seq_len, groups, block),
        preferred_element_type=jnp.float32,
    ).astype(jnp.bfloat16)
    qkv_parts = lax.all_to_all(qkv_term, "dp", 0, 0, tiled=True)
    sums = jnp.sum(qkv_parts.astype(jnp.float32), axis=0).T * scale_out
    query_grads = sums[:, :q_width][None]
    key_grads = sums[:, q_width : q_width + k_width][None]
    value_grads = sums[:, q_width + k_width :][None]
    return (saved_input[None], query_grads, key_grads, value_grads, output_grads[None])


def solution(mesh):
    placed = (
        P("pipe", ("dp", "tensor"), None),
        P("pipe", None),
        P("pipe", None, "tensor"),
        P("pipe", None, "tensor"),
        P("pipe", None, "tensor"),
        P("pipe", "tensor", None),
        P(("dp", "tensor"), None),
        P("dp", None),
    )
    return jax.shard_map(
        local,
        mesh=mesh,
        in_specs=placed,
        out_specs=(
            P("pipe", ("dp", "tensor"), None),
            P("pipe", "dp", "tensor"),
            P("pipe", "dp", "tensor"),
            P("pipe", "dp", "tensor"),
            P("pipe", "tensor", "dp"),
        ),
        check_vma=False,
    )
```

```python
import math

import jax
import jax.numpy as jnp
from jax import lax
from jax.sharding import PartitionSpec as P

HD = 128


epsilon = 1e-05
rope_base = 500000.0


def shifted(shard, axis, by):
    devices = lax.axis_size(axis)
    pairs = [(i, i + by) for i in range(devices) if 0 <= i + by < devices]
    return lax.ppermute(shard, axis, pairs)


def exchange_sum(blocks, axis, dim=0):
    devices = lax.axis_size(axis)
    me = lax.axis_index(axis)
    total = lax.dynamic_index_in_dim(blocks, me, axis=dim, keepdims=False).astype(jnp.float32)
    for by in range(1, devices):
        outgoing = lax.dynamic_index_in_dim(blocks, (me + by) % devices, axis=dim, keepdims=False)
        incoming = lax.ppermute(outgoing, axis, [(i, (i + by) % devices) for i in range(devices)])
        total = total + incoming.astype(jnp.float32)
    return total


def chip_pair_exchange_sum(blocks, axis):
    me = lax.axis_index(axis)
    pick = lambda index: lax.dynamic_index_in_dim(blocks, index, axis=0, keepdims=False)
    siblings = [(i, i ^ 1) for i in range(4)]
    for_pair = lax.ppermute(pick(me ^ 3), axis, siblings)
    pair = pick(me ^ 2).astype(jnp.float32) + for_pair.astype(jnp.float32)
    back = lax.ppermute(pair.astype(jnp.bfloat16), axis, [(i, i ^ 2) for i in range(4)])
    for_own = lax.ppermute(pick(me ^ 1), axis, siblings)
    own = pick(me).astype(jnp.float32) + for_own.astype(jnp.float32)
    return own + back.astype(jnp.float32)


def position_tables(document_ids, head_dim):
    seq_len = document_ids.shape[1]
    index = jnp.arange(seq_len, dtype=jnp.int32)
    earlier = (document_ids[:, None, :] < document_ids[:, :, None]).astype(jnp.int32)
    position = index[None, :] - jnp.sum(earlier, axis=2)
    half = head_dim // 2
    expo = jnp.arange(half, dtype=jnp.float32) * (2.0 / head_dim)
    freq = jnp.exp(expo * -math.log(rope_base))
    angle = position.astype(jnp.float32)[:, :, None] * freq
    same = document_ids[:, :, None] == document_ids[:, None, :]
    causal = index[:, None] >= index[None, :]
    visible = jnp.logical_and(same, causal[None])
    return (jnp.cos(angle), jnp.sin(angle), visible)


def rotate(vector, rot_cos, rot_sin, direction):
    half = vector.shape[-1] // 2
    first = vector[..., :half]
    second = vector[..., half:]
    return jnp.concatenate(
        [
            first * rot_cos - direction * second * rot_sin,
            second * rot_cos + direction * first * rot_sin,
        ],
        axis=-1,
    )


def normalize(rows, gain):
    values = rows.astype(jnp.float32)
    inverse = lax.rsqrt(jnp.mean(values * values, axis=-1, keepdims=True) + epsilon)
    unit_rows = values * inverse
    normed = (unit_rows * gain.astype(jnp.float32)).astype(jnp.bfloat16)
    return (inverse, unit_rows, normed)


def attention_forward(query_rot, key_rot, value_low, visible):
    scale = 1.0 / math.sqrt(HD)
    scores = (
        jnp.einsum("bqngd,bknd->bngqk", query_rot, key_rot, preferred_element_type=jnp.float32)
        * scale
    )
    expo = jnp.where(visible[:, None, None], jnp.exp(scores), 0.0)
    prob = expo / jnp.sum(expo, axis=-1, keepdims=True)
    prob_low = prob.astype(jnp.bfloat16)
    mixed = jnp.einsum("bngqk,bknd->bqngd", prob_low, value_low, preferred_element_type=jnp.float32)
    return (prob, prob_low, mixed.astype(jnp.bfloat16))


def attention_backward(grad_mixed, query_rot, key_rot, value_low, prob, prob_low, rot_cos, rot_sin):
    scale = 1.0 / math.sqrt(HD)
    grad_value = jnp.einsum(
        "bngqk,bqngd->bknd", prob_low, grad_mixed, preferred_element_type=jnp.float32
    )
    grad_prob = jnp.einsum(
        "bqngd,bknd->bngqk", grad_mixed, value_low, preferred_element_type=jnp.float32
    )
    grad_score = prob * (grad_prob - jnp.sum(grad_prob * prob, axis=-1, keepdims=True)) * scale
    score_low = grad_score.astype(jnp.bfloat16)
    grad_query = jnp.einsum(
        "bngqk,bknd->bqngd", score_low, key_rot, preferred_element_type=jnp.float32
    )
    grad_key = jnp.einsum(
        "bngqk,bqngd->bknd", score_low, query_rot, preferred_element_type=jnp.float32
    )
    grad_query = rotate(
        grad_query, rot_cos[:, :, None, None, :], rot_sin[:, :, None, None, :], -1.0
    )
    grad_key = rotate(grad_key, rot_cos[:, :, None, :], rot_sin[:, :, None, :], -1.0)
    return (
        grad_query.astype(jnp.bfloat16),
        grad_key.astype(jnp.bfloat16),
        grad_value.astype(jnp.bfloat16),
    )


def back_norm(grad_normed, unit_rows, inverse, gain, incoming):
    grad_unit = grad_normed * gain.astype(jnp.float32)
    branch = (
        grad_unit - unit_rows * jnp.mean(grad_unit * unit_rows, axis=-1, keepdims=True)
    ) * inverse
    return (incoming.astype(jnp.float32) + branch).astype(jnp.bfloat16)


def local(
    section_inputs,
    norm_gain,
    query_weight,
    key_weight,
    value_weight,
    output_weight,
    upstream_grad,
    document_ids,
):
    pipes = lax.axis_size("pipe")
    section = lax.axis_index("pipe")
    groups = lax.axis_size("dp")
    width = section_inputs.shape[2]
    seq_len = document_ids.shape[1]
    q_width = query_weight.shape[2]
    k_width = key_weight.shape[2]
    kv_local = k_width // HD
    group = q_width // k_width
    gain = norm_gain[0]
    w_query = query_weight[0]
    w_key = key_weight[0]
    w_value = value_weight[0]
    w_output = output_weight[0]
    rot_cos, rot_sin, visible = position_tables(document_ids, HD)
    last = pipes - 1
    inverse, unit_rows, normed_shard = normalize(section_inputs[0], gain)
    normed = lax.all_gather(normed_shard, "tensor", axis=0, tiled=True)
    incoming = jnp.where(section == last, upstream_grad, jnp.zeros_like(upstream_grad))
    query = jnp.dot(normed, w_query, preferred_element_type=jnp.float32).reshape(
        1, seq_len, kv_local, group, HD
    )
    keys = jnp.dot(normed, w_key, preferred_element_type=jnp.float32).reshape(
        1, seq_len, kv_local, HD
    )
    values = jnp.dot(normed, w_value, preferred_element_type=jnp.float32).reshape(
        1, seq_len, kv_local, HD
    )
    query_rot = rotate(
        query, rot_cos[:, :, None, None, :], rot_sin[:, :, None, None, :], 1.0
    ).astype(jnp.bfloat16)
    key_rot = rotate(keys, rot_cos[:, :, None, :], rot_sin[:, :, None, :], 1.0).astype(jnp.bfloat16)
    value_low = values.astype(jnp.bfloat16)
    prob, prob_low, mixed = attention_forward(query_rot, key_rot, value_low, visible)
    mixed_flat = mixed.reshape(seq_len, q_width)

    def backward_turn(cotangent):
        grad_mixed = jnp.einsum(
            "sd,hd->sh", cotangent, w_output, preferred_element_type=jnp.float32
        )
        grad_mixed = grad_mixed.astype(jnp.bfloat16).reshape(1, seq_len, kv_local, group, HD)
        grad_query, grad_key, grad_value = attention_backward(
            grad_mixed, query_rot, key_rot, value_low, prob, prob_low, rot_cos, rot_sin
        )
        flat_query = grad_query.reshape(seq_len, q_width)
        flat_key = grad_key.reshape(seq_len, k_width)
        flat_value = grad_value.reshape(seq_len, k_width)
        grad_normed = (
            jnp.einsum("sh,dh->sd", flat_query, w_query, preferred_element_type=jnp.float32)
            + jnp.einsum("sh,dh->sd", flat_key, w_key, preferred_element_type=jnp.float32)
            + jnp.einsum("sh,dh->sd", flat_value, w_value, preferred_element_type=jnp.float32)
        )
        return (grad_normed.astype(jnp.bfloat16), flat_query, flat_key, flat_value)

    def skipped_turn(cotangent):
        return (
            jnp.zeros((seq_len, width), jnp.bfloat16),
            jnp.zeros((seq_len, q_width), jnp.bfloat16),
            jnp.zeros((seq_len, k_width), jnp.bfloat16),
            jnp.zeros((seq_len, k_width), jnp.bfloat16),
        )

    saved_query = jnp.zeros((seq_len, q_width), jnp.bfloat16)
    saved_key = jnp.zeros((seq_len, k_width), jnp.bfloat16)
    saved_value = jnp.zeros((seq_len, k_width), jnp.bfloat16)
    saved_cot = jnp.zeros((seq_len, width), jnp.bfloat16)
    saved_input = jnp.zeros_like(incoming)
    for turn in range(pipes):
        active = section == last - turn
        cotangent = lax.all_gather(incoming, "tensor", axis=0, tiled=True)
        grad_normed, flat_query, flat_key, flat_value = lax.cond(
            active, backward_turn, skipped_turn, cotangent
        )
        tensors = lax.axis_size("tensor")
        grad_blocks = grad_normed.reshape(tensors, seq_len // tensors, width)
        if tensors == 4:
            summed = chip_pair_exchange_sum(grad_blocks, "tensor")
        else:
            summed = exchange_sum(grad_blocks, "tensor")
        result = back_norm(summed, unit_rows, inverse, gain, incoming)
        saved_query = jnp.where(active, flat_query, saved_query)
        saved_key = jnp.where(active, flat_key, saved_key)
        saved_value = jnp.where(active, flat_value, saved_value)
        saved_cot = jnp.where(active, cotangent, saved_cot)
        saved_input = jnp.where(active, result, saved_input)
        if turn + 1 < pipes:
            incoming = shifted(result, "pipe", -1)
    scale_out = 1.0 / math.sqrt(groups * seq_len)
    block = width // groups
    out_term = jnp.einsum(
        "sh,sjd->jhd",
        mixed_flat,
        saved_cot.reshape(seq_len, groups, block),
        preferred_element_type=jnp.float32,
    ).astype(jnp.bfloat16)
    out_parts = lax.all_to_all(out_term, "dp", 0, 0, tiled=True)
    output_grads = jnp.sum(out_parts.astype(jnp.float32), axis=0) * scale_out
    grads_qkv = jnp.concatenate([saved_query, saved_key, saved_value], axis=1)
    qkv_term = jnp.einsum(
        "sh,sjd->jhd",
        grads_qkv,
        normed.reshape(seq_len, groups, block),
        preferred_element_type=jnp.float32,
    ).astype(jnp.bfloat16)
    qkv_parts = lax.all_to_all(qkv_term, "dp", 0, 0, tiled=True)
    sums = jnp.sum(qkv_parts.astype(jnp.float32), axis=0).T * scale_out
    query_grads = sums[:, :q_width][None]
    key_grads = sums[:, q_width : q_width + k_width][None]
    value_grads = sums[:, q_width + k_width :][None]
    return (saved_input[None], query_grads, key_grads, value_grads, output_grads[None])


def solution(mesh):
    placed = (
        P("pipe", ("dp", "tensor"), None),
        P("pipe", None),
        P("pipe", None, "tensor"),
        P("pipe", None, "tensor"),
        P("pipe", None, "tensor"),
        P("pipe", "tensor", None),
        P(("dp", "tensor"), None),
        P("dp", None),
    )
    return jax.shard_map(
        local,
        mesh=mesh,
        in_specs=placed,
        out_specs=(
            P("pipe", ("dp", "tensor"), None),
            P("pipe", "dp", "tensor"),
            P("pipe", "dp", "tensor"),
            P("pipe", "dp", "tensor"),
            P("pipe", "tensor", "dp"),
        ),
        check_vma=False,
    )
```

```python
import math

import jax
import jax.numpy as jnp
from jax import lax
from jax.sharding import PartitionSpec as P

HD = 128


epsilon = 1e-05
rope_base = 500000.0


def shifted(shard, axis, by):
    devices = lax.axis_size(axis)
    pairs = [(i, i + by) for i in range(devices) if 0 <= i + by < devices]
    return lax.ppermute(shard, axis, pairs)


def exchange_sum(blocks, axis, dim=0):
    devices = lax.axis_size(axis)
    me = lax.axis_index(axis)
    total = lax.dynamic_index_in_dim(blocks, me, axis=dim, keepdims=False).astype(jnp.float32)
    for by in range(1, devices):
        outgoing = lax.dynamic_index_in_dim(blocks, (me + by) % devices, axis=dim, keepdims=False)
        incoming = lax.ppermute(outgoing, axis, [(i, (i + by) % devices) for i in range(devices)])
        total = total + incoming.astype(jnp.float32)
    return total


def chip_pair_exchange_sum(blocks, axis):
    me = lax.axis_index(axis)
    pick = lambda index: lax.dynamic_index_in_dim(blocks, index, axis=0, keepdims=False)
    siblings = [(i, i ^ 1) for i in range(4)]
    for_pair = lax.ppermute(pick(me ^ 3), axis, siblings)
    pair = pick(me ^ 2).astype(jnp.float32) + for_pair.astype(jnp.float32)
    back = lax.ppermute(pair.astype(jnp.bfloat16), axis, [(i, i ^ 2) for i in range(4)])
    for_own = lax.ppermute(pick(me ^ 1), axis, siblings)
    own = pick(me).astype(jnp.float32) + for_own.astype(jnp.float32)
    return own + back.astype(jnp.float32)


def position_tables(document_ids, head_dim):
    seq_len = document_ids.shape[1]
    index = jnp.arange(seq_len, dtype=jnp.int32)
    earlier = (document_ids[:, None, :] < document_ids[:, :, None]).astype(jnp.int32)
    position = index[None, :] - jnp.sum(earlier, axis=2)
    half = head_dim // 2
    expo = jnp.arange(half, dtype=jnp.float32) * (2.0 / head_dim)
    freq = jnp.exp(expo * -math.log(rope_base))
    angle = position.astype(jnp.float32)[:, :, None] * freq
    same = document_ids[:, :, None] == document_ids[:, None, :]
    causal = index[:, None] >= index[None, :]
    visible = jnp.logical_and(same, causal[None])
    return (jnp.cos(angle), jnp.sin(angle), visible)


def rotate(vector, rot_cos, rot_sin, direction):
    half = vector.shape[-1] // 2
    first = vector[..., :half]
    second = vector[..., half:]
    return jnp.concatenate(
        [
            first * rot_cos - direction * second * rot_sin,
            second * rot_cos + direction * first * rot_sin,
        ],
        axis=-1,
    )


def normalize(rows, gain):
    values = rows.astype(jnp.float32)
    inverse = lax.rsqrt(jnp.mean(values * values, axis=-1, keepdims=True) + epsilon)
    unit_rows = values * inverse
    normed = (unit_rows * gain.astype(jnp.float32)).astype(jnp.bfloat16)
    return (inverse, unit_rows, normed)


def attention_forward(query_rot, key_rot, value_low, visible):
    scale = 1.0 / math.sqrt(HD)
    scores = (
        jnp.einsum("bqngd,bknd->bngqk", query_rot, key_rot, preferred_element_type=jnp.float32)
        * scale
    )
    expo = jnp.where(visible[:, None, None], jnp.exp(scores), 0.0)
    prob = expo / jnp.sum(expo, axis=-1, keepdims=True)
    prob_low = prob.astype(jnp.bfloat16)
    mixed = jnp.einsum("bngqk,bknd->bqngd", prob_low, value_low, preferred_element_type=jnp.float32)
    return (prob, prob_low, mixed.astype(jnp.bfloat16))


def attention_backward(grad_mixed, query_rot, key_rot, value_low, prob, prob_low, rot_cos, rot_sin):
    scale = 1.0 / math.sqrt(HD)
    grad_value = jnp.einsum(
        "bnqgk,bqngd->bknd", prob_low, grad_mixed, preferred_element_type=jnp.float32
    )
    grad_prob = jnp.einsum(
        "bqngd,bknd->bngqk", grad_mixed, value_low, preferred_element_type=jnp.float32
    )
    grad_score = prob * (grad_prob - jnp.sum(grad_prob * prob, axis=-1, keepdims=True)) * scale
    score_low = grad_score.astype(jnp.bfloat16)
    grad_query = jnp.einsum(
        "bngqk,bknd->bqngd", score_low, key_rot, preferred_element_type=jnp.float32
    )
    grad_key = jnp.einsum(
        "bngqk,bqngd->bknd", score_low, query_rot, preferred_element_type=jnp.float32
    )
    grad_query = rotate(
        grad_query, rot_cos[:, :, None, None, :], rot_sin[:, :, None, None, :], -1.0
    )
    grad_key = rotate(grad_key, rot_cos[:, :, None, :], rot_sin[:, :, None, :], -1.0)
    return (
        grad_query.astype(jnp.bfloat16),
        grad_key.astype(jnp.bfloat16),
        grad_value.astype(jnp.bfloat16),
    )


def back_norm(grad_normed, unit_rows, inverse, gain, incoming):
    grad_unit = grad_normed * gain.astype(jnp.float32)
    branch = (
        grad_unit - unit_rows * jnp.mean(grad_unit * unit_rows, axis=-1, keepdims=True)
    ) * inverse
    return (incoming.astype(jnp.float32) + branch).astype(jnp.bfloat16)


def local(
    section_inputs,
    norm_gain,
    query_weight,
    key_weight,
    value_weight,
    output_weight,
    upstream_grad,
    document_ids,
):
    pipes = lax.axis_size("pipe")
    section = lax.axis_index("pipe")
    groups = lax.axis_size("dp")
    width = section_inputs.shape[2]
    seq_len = document_ids.shape[1]
    q_width = query_weight.shape[2]
    k_width = key_weight.shape[2]
    kv_local = k_width // HD
    group = q_width // k_width
    gain = norm_gain[0]
    w_query = query_weight[0]
    w_key = key_weight[0]
    w_value = value_weight[0]
    w_output = output_weight[0]
    rot_cos, rot_sin, visible = position_tables(document_ids, HD)
    last = pipes - 1
    inverse, unit_rows, normed_shard = normalize(section_inputs[0], gain)
    normed = lax.all_gather(normed_shard, "tensor", axis=0, tiled=True)
    incoming = jnp.where(section == last, upstream_grad, jnp.zeros_like(upstream_grad))
    query = jnp.dot(normed, w_query, preferred_element_type=jnp.float32).reshape(
        1, seq_len, kv_local, group, HD
    )
    keys = jnp.dot(normed, w_key, preferred_element_type=jnp.float32).reshape(
        1, seq_len, kv_local, HD
    )
    values = jnp.dot(normed, w_value, preferred_element_type=jnp.float32).reshape(
        1, seq_len, kv_local, HD
    )
    query_rot = rotate(
        query, rot_cos[:, :, None, None, :], rot_sin[:, :, None, None, :], 1.0
    ).astype(jnp.bfloat16)
    key_rot = rotate(keys, rot_cos[:, :, None, :], rot_sin[:, :, None, :], 1.0).astype(jnp.bfloat16)
    value_low = values.astype(jnp.bfloat16)
    prob, prob_low, mixed = attention_forward(query_rot, key_rot, value_low, visible)
    prob_low = lax.optimization_barrier(jnp.transpose(prob_low, (0, 1, 3, 2, 4)))
    mixed_flat = mixed.reshape(seq_len, q_width)

    def backward_turn(cotangent):
        grad_mixed = jnp.einsum(
            "sd,hd->sh", cotangent, w_output, preferred_element_type=jnp.float32
        )
        grad_mixed = grad_mixed.astype(jnp.bfloat16).reshape(1, seq_len, kv_local, group, HD)
        grad_query, grad_key, grad_value = attention_backward(
            grad_mixed, query_rot, key_rot, value_low, prob, prob_low, rot_cos, rot_sin
        )
        flat_query = grad_query.reshape(seq_len, q_width)
        flat_key = grad_key.reshape(seq_len, k_width)
        flat_value = grad_value.reshape(seq_len, k_width)
        grad_normed = (
            jnp.einsum("sh,dh->sd", flat_query, w_query, preferred_element_type=jnp.float32)
            + jnp.einsum("sh,dh->sd", flat_key, w_key, preferred_element_type=jnp.float32)
            + jnp.einsum("sh,dh->sd", flat_value, w_value, preferred_element_type=jnp.float32)
        )
        return (grad_normed.astype(jnp.bfloat16), flat_query, flat_key, flat_value)

    def skipped_turn(cotangent):
        return (
            jnp.zeros((seq_len, width), jnp.bfloat16),
            jnp.zeros((seq_len, q_width), jnp.bfloat16),
            jnp.zeros((seq_len, k_width), jnp.bfloat16),
            jnp.zeros((seq_len, k_width), jnp.bfloat16),
        )

    saved_query = jnp.zeros((seq_len, q_width), jnp.bfloat16)
    saved_key = jnp.zeros((seq_len, k_width), jnp.bfloat16)
    saved_value = jnp.zeros((seq_len, k_width), jnp.bfloat16)
    saved_cot = jnp.zeros((seq_len, width), jnp.bfloat16)
    saved_input = jnp.zeros_like(incoming)
    for turn in range(pipes):
        active = section == last - turn
        cotangent = lax.all_gather(incoming, "tensor", axis=0, tiled=True)
        grad_normed, flat_query, flat_key, flat_value = lax.cond(
            active, backward_turn, skipped_turn, cotangent
        )
        tensors = lax.axis_size("tensor")
        grad_blocks = grad_normed.reshape(tensors, seq_len // tensors, width)
        if tensors == 4:
            summed = chip_pair_exchange_sum(grad_blocks, "tensor")
        else:
            summed = exchange_sum(grad_blocks, "tensor")
        result = back_norm(summed, unit_rows, inverse, gain, incoming)
        saved_query = jnp.where(active, flat_query, saved_query)
        saved_key = jnp.where(active, flat_key, saved_key)
        saved_value = jnp.where(active, flat_value, saved_value)
        saved_cot = jnp.where(active, cotangent, saved_cot)
        saved_input = jnp.where(active, result, saved_input)
        if turn + 1 < pipes:
            incoming = shifted(result, "pipe", -1)
    scale_out = 1.0 / math.sqrt(groups * seq_len)
    block = width // groups
    out_term = jnp.einsum(
        "sh,sjd->jhd",
        mixed_flat,
        saved_cot.reshape(seq_len, groups, block),
        preferred_element_type=jnp.float32,
    ).astype(jnp.bfloat16)
    out_parts = lax.all_to_all(out_term, "dp", 0, 0, tiled=True)
    output_grads = jnp.sum(out_parts.astype(jnp.float32), axis=0) * scale_out
    grads_qkv = jnp.concatenate([saved_query, saved_key, saved_value], axis=1)
    qkv_term = jnp.einsum(
        "sh,sjd->jhd",
        grads_qkv,
        normed.reshape(seq_len, groups, block),
        preferred_element_type=jnp.float32,
    ).astype(jnp.bfloat16)
    qkv_parts = lax.all_to_all(qkv_term, "dp", 0, 0, tiled=True)
    sums = jnp.sum(qkv_parts.astype(jnp.float32), axis=0).T * scale_out
    query_grads = sums[:, :q_width][None]
    key_grads = sums[:, q_width : q_width + k_width][None]
    value_grads = sums[:, q_width + k_width :][None]
    return (saved_input[None], query_grads, key_grads, value_grads, output_grads[None])


def solution(mesh):
    placed = (
        P("pipe", ("dp", "tensor"), None),
        P("pipe", None),
        P("pipe", None, "tensor"),
        P("pipe", None, "tensor"),
        P("pipe", None, "tensor"),
        P("pipe", "tensor", None),
        P(("dp", "tensor"), None),
        P("dp", None),
    )
    return jax.shard_map(
        local,
        mesh=mesh,
        in_specs=placed,
        out_specs=(
            P("pipe", ("dp", "tensor"), None),
            P("pipe", "dp", "tensor"),
            P("pipe", "dp", "tensor"),
            P("pipe", "dp", "tensor"),
            P("pipe", "tensor", "dp"),
        ),
        check_vma=False,
    )
```

```python
import math

import jax
import jax.numpy as jnp
from jax import lax
from jax.sharding import PartitionSpec as P

HD = 128


epsilon = 1e-05
rope_base = 500000.0


def shifted(shard, axis, by):
    devices = lax.axis_size(axis)
    pairs = [(i, i + by) for i in range(devices) if 0 <= i + by < devices]
    return lax.ppermute(shard, axis, pairs)


def exchange_sum(blocks, axis, dim=0):
    devices = lax.axis_size(axis)
    me = lax.axis_index(axis)
    total = lax.dynamic_index_in_dim(blocks, me, axis=dim, keepdims=False).astype(jnp.float32)
    for by in range(1, devices):
        outgoing = lax.dynamic_index_in_dim(blocks, (me + by) % devices, axis=dim, keepdims=False)
        incoming = lax.ppermute(outgoing, axis, [(i, (i + by) % devices) for i in range(devices)])
        total = total + incoming.astype(jnp.float32)
    return total


def chip_pair_exchange_sum(blocks, axis):
    me = lax.axis_index(axis)
    pick = lambda index: lax.dynamic_index_in_dim(blocks, index, axis=0, keepdims=False)
    siblings = [(i, i ^ 1) for i in range(4)]
    for_pair = lax.ppermute(pick(me ^ 3), axis, siblings)
    pair = pick(me ^ 2).astype(jnp.float32) + for_pair.astype(jnp.float32)
    back = lax.ppermute(pair.astype(jnp.bfloat16), axis, [(i, i ^ 2) for i in range(4)])
    for_own = lax.ppermute(pick(me ^ 1), axis, siblings)
    own = pick(me).astype(jnp.float32) + for_own.astype(jnp.float32)
    return own + back.astype(jnp.float32)


def chip_pair_gather(rows, axis):
    me = lax.axis_index(axis)
    other = lax.ppermute(rows, axis, [(i, i ^ 2) for i in range(4)])
    mine = jnp.stack([rows, other])
    theirs = lax.ppermute(mine, axis, [(i, i ^ 1) for i in range(4)])
    core = me % 2
    low = jnp.where(core == 0, mine, theirs)
    high = jnp.where(core == 0, theirs, mine)
    chip_first = jnp.stack([low[0], high[0], low[1], high[1]])
    chip_second = jnp.stack([low[1], high[1], low[0], high[0]])
    ordered = jnp.where(me // 2 == 0, chip_first, chip_second)
    return ordered.reshape(4 * rows.shape[0], rows.shape[1])


def position_tables(document_ids, head_dim):
    seq_len = document_ids.shape[1]
    index = jnp.arange(seq_len, dtype=jnp.int32)
    earlier = (document_ids[:, None, :] < document_ids[:, :, None]).astype(jnp.int32)
    position = index[None, :] - jnp.sum(earlier, axis=2)
    half = head_dim // 2
    expo = jnp.arange(half, dtype=jnp.float32) * (2.0 / head_dim)
    freq = jnp.exp(expo * -math.log(rope_base))
    angle = position.astype(jnp.float32)[:, :, None] * freq
    same = document_ids[:, :, None] == document_ids[:, None, :]
    causal = index[:, None] >= index[None, :]
    visible = jnp.logical_and(same, causal[None])
    return (jnp.cos(angle), jnp.sin(angle), visible)


def rotate(vector, rot_cos, rot_sin, direction):
    half = vector.shape[-1] // 2
    first = vector[..., :half]
    second = vector[..., half:]
    return jnp.concatenate(
        [
            first * rot_cos - direction * second * rot_sin,
            second * rot_cos + direction * first * rot_sin,
        ],
        axis=-1,
    )


def normalize(rows, gain):
    values = rows.astype(jnp.float32)
    inverse = lax.rsqrt(jnp.mean(values * values, axis=-1, keepdims=True) + epsilon)
    unit_rows = values * inverse
    normed = (unit_rows * gain.astype(jnp.float32)).astype(jnp.bfloat16)
    return (inverse, unit_rows, normed)


def attention_forward(query_rot, key_rot, value_low, visible):
    scale = 1.0 / math.sqrt(HD)
    scores = (
        jnp.einsum("bqngd,bknd->bngqk", query_rot, key_rot, preferred_element_type=jnp.float32)
        * scale
    )
    expo = jnp.where(visible[:, None, None], jnp.exp(scores), 0.0)
    prob = expo / jnp.sum(expo, axis=-1, keepdims=True)
    prob_low = prob.astype(jnp.bfloat16)
    mixed = jnp.einsum("bngqk,bknd->bqngd", prob_low, value_low, preferred_element_type=jnp.float32)
    return (prob, prob_low, mixed.astype(jnp.bfloat16))


def attention_backward(grad_mixed, query_rot, key_rot, value_low, prob, prob_low, rot_cos, rot_sin):
    scale = 1.0 / math.sqrt(HD)
    grad_value = jnp.einsum(
        "bnqgk,bqngd->bknd", prob_low, grad_mixed, preferred_element_type=jnp.float32
    )
    grad_prob = jnp.einsum(
        "bqngd,bknd->bngqk", grad_mixed, value_low, preferred_element_type=jnp.float32
    )
    grad_score = prob * (grad_prob - jnp.sum(grad_prob * prob, axis=-1, keepdims=True)) * scale
    score_low = grad_score.astype(jnp.bfloat16)
    grad_query = jnp.einsum(
        "bngqk,bknd->bqngd", score_low, key_rot, preferred_element_type=jnp.float32
    )
    grad_key = jnp.einsum(
        "bngqk,bqngd->bknd", score_low, query_rot, preferred_element_type=jnp.float32
    )
    grad_query = rotate(
        grad_query, rot_cos[:, :, None, None, :], rot_sin[:, :, None, None, :], -1.0
    )
    grad_key = rotate(grad_key, rot_cos[:, :, None, :], rot_sin[:, :, None, :], -1.0)
    return (
        grad_query.astype(jnp.bfloat16),
        grad_key.astype(jnp.bfloat16),
        grad_value.astype(jnp.bfloat16),
    )


def back_norm(grad_normed, unit_rows, inverse, gain, incoming):
    grad_unit = grad_normed * gain.astype(jnp.float32)
    branch = (
        grad_unit - unit_rows * jnp.mean(grad_unit * unit_rows, axis=-1, keepdims=True)
    ) * inverse
    return (incoming.astype(jnp.float32) + branch).astype(jnp.bfloat16)


def local(
    section_inputs,
    norm_gain,
    query_weight,
    key_weight,
    value_weight,
    output_weight,
    upstream_grad,
    document_ids,
):
    pipes = lax.axis_size("pipe")
    section = lax.axis_index("pipe")
    groups = lax.axis_size("dp")
    width = section_inputs.shape[2]
    seq_len = document_ids.shape[1]
    q_width = query_weight.shape[2]
    k_width = key_weight.shape[2]
    kv_local = k_width // HD
    group = q_width // k_width
    gain = norm_gain[0]
    w_query = query_weight[0]
    w_key = key_weight[0]
    w_value = value_weight[0]
    w_output = output_weight[0]
    rot_cos, rot_sin, visible = position_tables(document_ids, HD)
    last = pipes - 1
    inverse, unit_rows, normed_shard = normalize(section_inputs[0], gain)
    normed = lax.all_gather(normed_shard, "tensor", axis=0, tiled=True)
    incoming = jnp.where(section == last, upstream_grad, jnp.zeros_like(upstream_grad))
    query = jnp.dot(normed, w_query, preferred_element_type=jnp.float32).reshape(
        1, seq_len, kv_local, group, HD
    )
    keys = jnp.dot(normed, w_key, preferred_element_type=jnp.float32).reshape(
        1, seq_len, kv_local, HD
    )
    values = jnp.dot(normed, w_value, preferred_element_type=jnp.float32).reshape(
        1, seq_len, kv_local, HD
    )
    query_rot = rotate(
        query, rot_cos[:, :, None, None, :], rot_sin[:, :, None, None, :], 1.0
    ).astype(jnp.bfloat16)
    key_rot = rotate(keys, rot_cos[:, :, None, :], rot_sin[:, :, None, :], 1.0).astype(jnp.bfloat16)
    value_low = values.astype(jnp.bfloat16)
    prob, prob_low, mixed = attention_forward(query_rot, key_rot, value_low, visible)
    prob_low = lax.optimization_barrier(jnp.transpose(prob_low, (0, 1, 3, 2, 4)))
    mixed_flat = mixed.reshape(seq_len, q_width)

    def backward_turn(cotangent):
        grad_mixed = jnp.einsum(
            "sd,hd->sh", cotangent, w_output, preferred_element_type=jnp.float32
        )
        grad_mixed = grad_mixed.astype(jnp.bfloat16).reshape(1, seq_len, kv_local, group, HD)
        grad_query, grad_key, grad_value = attention_backward(
            grad_mixed, query_rot, key_rot, value_low, prob, prob_low, rot_cos, rot_sin
        )
        flat_query = grad_query.reshape(seq_len, q_width)
        flat_key = grad_key.reshape(seq_len, k_width)
        flat_value = grad_value.reshape(seq_len, k_width)
        grad_normed = (
            jnp.einsum("sh,dh->sd", flat_query, w_query, preferred_element_type=jnp.float32)
            + jnp.einsum("sh,dh->sd", flat_key, w_key, preferred_element_type=jnp.float32)
            + jnp.einsum("sh,dh->sd", flat_value, w_value, preferred_element_type=jnp.float32)
        )
        return (grad_normed.astype(jnp.bfloat16), flat_query, flat_key, flat_value)

    def skipped_turn(cotangent):
        return (
            jnp.zeros((seq_len, width), jnp.bfloat16),
            jnp.zeros((seq_len, q_width), jnp.bfloat16),
            jnp.zeros((seq_len, k_width), jnp.bfloat16),
            jnp.zeros((seq_len, k_width), jnp.bfloat16),
        )

    saved_query = jnp.zeros((seq_len, q_width), jnp.bfloat16)
    saved_key = jnp.zeros((seq_len, k_width), jnp.bfloat16)
    saved_value = jnp.zeros((seq_len, k_width), jnp.bfloat16)
    saved_cot = jnp.zeros((seq_len, width), jnp.bfloat16)
    saved_input = jnp.zeros_like(incoming)
    for turn in range(pipes):
        active = section == last - turn
        if turn == 0 and lax.axis_size("tensor") == 4:
            cotangent = chip_pair_gather(incoming, "tensor")
        else:
            cotangent = lax.all_gather(incoming, "tensor", axis=0, tiled=True)
        grad_normed, flat_query, flat_key, flat_value = lax.cond(
            active, backward_turn, skipped_turn, cotangent
        )
        tensors = lax.axis_size("tensor")
        grad_blocks = grad_normed.reshape(tensors, seq_len // tensors, width)
        if tensors == 4:
            summed = chip_pair_exchange_sum(grad_blocks, "tensor")
        else:
            summed = exchange_sum(grad_blocks, "tensor")
        result = back_norm(summed, unit_rows, inverse, gain, incoming)
        saved_query = jnp.where(active, flat_query, saved_query)
        saved_key = jnp.where(active, flat_key, saved_key)
        saved_value = jnp.where(active, flat_value, saved_value)
        saved_cot = jnp.where(active, cotangent, saved_cot)
        saved_input = jnp.where(active, result, saved_input)
        if turn + 1 < pipes:
            incoming = shifted(result, "pipe", -1)
    scale_out = 1.0 / math.sqrt(groups * seq_len)
    block = width // groups
    out_term = jnp.einsum(
        "sh,sjd->jhd",
        mixed_flat,
        saved_cot.reshape(seq_len, groups, block),
        preferred_element_type=jnp.float32,
    ).astype(jnp.bfloat16)
    out_parts = lax.all_to_all(out_term, "dp", 0, 0, tiled=True)
    output_grads = jnp.sum(out_parts.astype(jnp.float32), axis=0) * scale_out
    grads_qkv = jnp.concatenate([saved_query, saved_key, saved_value], axis=1)
    qkv_term = jnp.einsum(
        "sh,sjd->jhd",
        grads_qkv,
        normed.reshape(seq_len, groups, block),
        preferred_element_type=jnp.float32,
    ).astype(jnp.bfloat16)
    qkv_parts = lax.all_to_all(qkv_term, "dp", 0, 0, tiled=True)
    sums = jnp.sum(qkv_parts.astype(jnp.float32), axis=0).T * scale_out
    query_grads = sums[:, :q_width][None]
    key_grads = sums[:, q_width : q_width + k_width][None]
    value_grads = sums[:, q_width + k_width :][None]
    return (saved_input[None], query_grads, key_grads, value_grads, output_grads[None])


def solution(mesh):
    placed = (
        P("pipe", ("dp", "tensor"), None),
        P("pipe", None),
        P("pipe", None, "tensor"),
        P("pipe", None, "tensor"),
        P("pipe", None, "tensor"),
        P("pipe", "tensor", None),
        P(("dp", "tensor"), None),
        P("dp", None),
    )
    return jax.shard_map(
        local,
        mesh=mesh,
        in_specs=placed,
        out_specs=(
            P("pipe", ("dp", "tensor"), None),
            P("pipe", "dp", "tensor"),
            P("pipe", "dp", "tensor"),
            P("pipe", "dp", "tensor"),
            P("pipe", "tensor", "dp"),
        ),
        check_vma=False,
    )
```

```python
import math

import jax
import jax.numpy as jnp
from jax import lax
from jax.sharding import PartitionSpec as P

HD = 128


epsilon = 1e-05
rope_base = 500000.0


def shifted(shard, axis, by):
    devices = lax.axis_size(axis)
    pairs = [(i, i + by) for i in range(devices) if 0 <= i + by < devices]
    return lax.ppermute(shard, axis, pairs)


def exchange_sum(blocks, axis, dim=0):
    devices = lax.axis_size(axis)
    me = lax.axis_index(axis)
    total = lax.dynamic_index_in_dim(blocks, me, axis=dim, keepdims=False).astype(jnp.float32)
    for by in range(1, devices):
        outgoing = lax.dynamic_index_in_dim(blocks, (me + by) % devices, axis=dim, keepdims=False)
        incoming = lax.ppermute(outgoing, axis, [(i, (i + by) % devices) for i in range(devices)])
        total = total + incoming.astype(jnp.float32)
    return total


def chip_pair_exchange_sum(blocks, axis):
    me = lax.axis_index(axis)
    pick = lambda index: lax.dynamic_index_in_dim(blocks, index, axis=0, keepdims=False)
    siblings = [(i, i ^ 1) for i in range(4)]
    for_pair = lax.ppermute(pick(me ^ 3), axis, siblings)
    pair = pick(me ^ 2).astype(jnp.float32) + for_pair.astype(jnp.float32)
    back = lax.ppermute(pair.astype(jnp.bfloat16), axis, [(i, i ^ 2) for i in range(4)])
    for_own = lax.ppermute(pick(me ^ 1), axis, siblings)
    own = pick(me).astype(jnp.float32) + for_own.astype(jnp.float32)
    return own + back.astype(jnp.float32)


def position_tables(document_ids, head_dim):
    seq_len = document_ids.shape[1]
    index = jnp.arange(seq_len, dtype=jnp.int32)
    earlier = (document_ids[:, None, :] < document_ids[:, :, None]).astype(jnp.int32)
    position = index[None, :] - jnp.sum(earlier, axis=2)
    half = head_dim // 2
    expo = jnp.arange(half, dtype=jnp.float32) * (2.0 / head_dim)
    freq = jnp.exp(expo * -math.log(rope_base))
    angle = position.astype(jnp.float32)[:, :, None] * freq
    same = document_ids[:, :, None] == document_ids[:, None, :]
    causal = index[:, None] >= index[None, :]
    visible = jnp.logical_and(same, causal[None])
    return (jnp.cos(angle), jnp.sin(angle), visible)


def rotate(vector, rot_cos, rot_sin, direction):
    half = vector.shape[-1] // 2
    first = vector[..., :half]
    second = vector[..., half:]
    return jnp.concatenate(
        [
            first * rot_cos - direction * second * rot_sin,
            second * rot_cos + direction * first * rot_sin,
        ],
        axis=-1,
    )


def normalize(rows, gain):
    values = rows.astype(jnp.float32)
    inverse = lax.rsqrt(jnp.mean(values * values, axis=-1, keepdims=True) + epsilon)
    unit_rows = values * inverse
    normed = (unit_rows * gain.astype(jnp.float32)).astype(jnp.bfloat16)
    return (inverse, unit_rows, normed)


def attention_forward(query_rot, key_rot, value_low, visible):
    scale = 1.0 / math.sqrt(HD)
    scores = (
        jnp.einsum("bqngd,bknd->bngqk", query_rot, key_rot, preferred_element_type=jnp.float32)
        * scale
    )
    expo = jnp.where(visible[:, None, None], jnp.exp(scores), 0.0)
    prob = expo / jnp.sum(expo, axis=-1, keepdims=True)
    prob_low = prob.astype(jnp.bfloat16)
    mixed = jnp.einsum("bngqk,bknd->bqngd", prob_low, value_low, preferred_element_type=jnp.float32)
    return (prob, prob_low, mixed.astype(jnp.bfloat16))


def attention_backward(grad_mixed, query_rot, key_rot, value_low, prob, prob_low, rot_cos, rot_sin):
    scale = 1.0 / math.sqrt(HD)
    grad_value = jnp.einsum(
        "bngqk,bqngd->bknd", prob_low, grad_mixed, preferred_element_type=jnp.float32
    )
    grad_prob = jnp.einsum(
        "bqngd,bknd->bngqk", grad_mixed, value_low, preferred_element_type=jnp.float32
    )
    grad_score = prob * (grad_prob - jnp.sum(grad_prob * prob, axis=-1, keepdims=True)) * scale
    score_low = grad_score.astype(jnp.bfloat16)
    grad_query = jnp.einsum(
        "bngqk,bknd->bqngd", score_low, key_rot, preferred_element_type=jnp.float32
    )
    grad_key = jnp.einsum(
        "bngqk,bqngd->bknd", score_low, query_rot, preferred_element_type=jnp.float32
    )
    grad_query = rotate(
        grad_query, rot_cos[:, :, None, None, :], rot_sin[:, :, None, None, :], -1.0
    )
    grad_key = rotate(grad_key, rot_cos[:, :, None, :], rot_sin[:, :, None, :], -1.0)
    return (
        grad_query.astype(jnp.bfloat16),
        grad_key.astype(jnp.bfloat16),
        grad_value.astype(jnp.bfloat16),
    )


def back_norm(grad_normed, unit_rows, inverse, gain, incoming):
    grad_unit = grad_normed * gain.astype(jnp.float32)
    branch = (
        grad_unit - unit_rows * jnp.mean(grad_unit * unit_rows, axis=-1, keepdims=True)
    ) * inverse
    return (incoming.astype(jnp.float32) + branch).astype(jnp.bfloat16)


def local(
    section_inputs,
    norm_gain,
    query_weight,
    key_weight,
    value_weight,
    output_weight,
    upstream_grad,
    document_ids,
):
    pipes = lax.axis_size("pipe")
    section = lax.axis_index("pipe")
    groups = lax.axis_size("dp")
    width = section_inputs.shape[2]
    seq_len = document_ids.shape[1]
    q_width = query_weight.shape[2]
    k_width = key_weight.shape[2]
    kv_local = k_width // HD
    group = q_width // k_width
    gain = norm_gain[0]
    w_query = query_weight[0]
    w_key = key_weight[0]
    w_value = value_weight[0]
    w_output = output_weight[0]
    rot_cos, rot_sin, visible = position_tables(document_ids, HD)
    last = pipes - 1
    inverse, unit_rows, normed_shard = normalize(section_inputs[0], gain)
    normed = lax.all_gather(normed_shard, "tensor", axis=0, tiled=True)
    incoming = jnp.where(section == last, upstream_grad, jnp.zeros_like(upstream_grad))
    query = jnp.dot(normed, w_query, preferred_element_type=jnp.float32).reshape(
        1, seq_len, kv_local, group, HD
    )
    keys = jnp.dot(normed, w_key, preferred_element_type=jnp.float32).reshape(
        1, seq_len, kv_local, HD
    )
    values = jnp.dot(normed, w_value, preferred_element_type=jnp.float32).reshape(
        1, seq_len, kv_local, HD
    )
    query_rot = rotate(
        query, rot_cos[:, :, None, None, :], rot_sin[:, :, None, None, :], 1.0
    ).astype(jnp.bfloat16)
    key_rot = rotate(keys, rot_cos[:, :, None, :], rot_sin[:, :, None, :], 1.0).astype(jnp.bfloat16)
    value_low = values.astype(jnp.bfloat16)
    prob, prob_low, mixed = attention_forward(query_rot, key_rot, value_low, visible)
    mixed_rows = lax.optimization_barrier(mixed.reshape(seq_len, q_width).T)

    def backward_turn(cotangent):
        grad_mixed = jnp.einsum(
            "sd,hd->sh", cotangent, w_output, preferred_element_type=jnp.float32
        )
        grad_mixed = grad_mixed.astype(jnp.bfloat16).reshape(1, seq_len, kv_local, group, HD)
        grad_query, grad_key, grad_value = attention_backward(
            grad_mixed, query_rot, key_rot, value_low, prob, prob_low, rot_cos, rot_sin
        )
        flat_query = grad_query.reshape(seq_len, q_width)
        flat_key = grad_key.reshape(seq_len, k_width)
        flat_value = grad_value.reshape(seq_len, k_width)
        grad_normed = (
            jnp.einsum("sh,dh->sd", flat_query, w_query, preferred_element_type=jnp.float32)
            + jnp.einsum("sh,dh->sd", flat_key, w_key, preferred_element_type=jnp.float32)
            + jnp.einsum("sh,dh->sd", flat_value, w_value, preferred_element_type=jnp.float32)
        )
        return (grad_normed.astype(jnp.bfloat16), flat_query, flat_key, flat_value)

    def skipped_turn(cotangent):
        return (
            jnp.zeros((seq_len, width), jnp.bfloat16),
            jnp.zeros((seq_len, q_width), jnp.bfloat16),
            jnp.zeros((seq_len, k_width), jnp.bfloat16),
            jnp.zeros((seq_len, k_width), jnp.bfloat16),
        )

    saved_query = jnp.zeros((seq_len, q_width), jnp.bfloat16)
    saved_key = jnp.zeros((seq_len, k_width), jnp.bfloat16)
    saved_value = jnp.zeros((seq_len, k_width), jnp.bfloat16)
    saved_cot = jnp.zeros((seq_len, width), jnp.bfloat16)
    saved_input = jnp.zeros_like(incoming)
    for turn in range(pipes):
        active = section == last - turn
        cotangent = lax.all_gather(incoming, "tensor", axis=0, tiled=True)
        grad_normed, flat_query, flat_key, flat_value = lax.cond(
            active, backward_turn, skipped_turn, cotangent
        )
        tensors = lax.axis_size("tensor")
        grad_blocks = grad_normed.reshape(tensors, seq_len // tensors, width)
        if tensors == 4:
            summed = chip_pair_exchange_sum(grad_blocks, "tensor")
        else:
            summed = exchange_sum(grad_blocks, "tensor")
        result = back_norm(summed, unit_rows, inverse, gain, incoming)
        saved_query = jnp.where(active, flat_query, saved_query)
        saved_key = jnp.where(active, flat_key, saved_key)
        saved_value = jnp.where(active, flat_value, saved_value)
        saved_cot = jnp.where(active, cotangent, saved_cot)
        saved_input = jnp.where(active, result, saved_input)
        if turn + 1 < pipes:
            incoming = shifted(result, "pipe", -1)
    scale_out = 1.0 / math.sqrt(groups * seq_len)
    block = width // groups
    out_term = jnp.dot(mixed_rows, saved_cot, preferred_element_type=jnp.float32).astype(jnp.bfloat16)
    out_parts = lax.all_to_all(out_term.reshape(q_width, groups, block), "dp", 1, 1, tiled=True)
    output_grads = jnp.sum(out_parts.astype(jnp.float32), axis=1) * scale_out
    grads_qkv = jnp.concatenate([saved_query, saved_key, saved_value], axis=1)
    qkv_term = jnp.einsum(
        "sh,sjd->jhd",
        grads_qkv,
        normed.reshape(seq_len, groups, block),
        preferred_element_type=jnp.float32,
    ).astype(jnp.bfloat16)
    qkv_parts = lax.all_to_all(qkv_term, "dp", 0, 0, tiled=True)
    sums = jnp.sum(qkv_parts.astype(jnp.float32), axis=0).T * scale_out
    query_grads = sums[:, :q_width][None]
    key_grads = sums[:, q_width : q_width + k_width][None]
    value_grads = sums[:, q_width + k_width :][None]
    return (saved_input[None], query_grads, key_grads, value_grads, output_grads[None])


def solution(mesh):
    placed = (
        P("pipe", ("dp", "tensor"), None),
        P("pipe", None),
        P("pipe", None, "tensor"),
        P("pipe", None, "tensor"),
        P("pipe", None, "tensor"),
        P("pipe", "tensor", None),
        P(("dp", "tensor"), None),
        P("dp", None),
    )
    return jax.shard_map(
        local,
        mesh=mesh,
        in_specs=placed,
        out_specs=(
            P("pipe", ("dp", "tensor"), None),
            P("pipe", "dp", "tensor"),
            P("pipe", "dp", "tensor"),
            P("pipe", "dp", "tensor"),
            P("pipe", "tensor", "dp"),
        ),
        check_vma=False,
    )
```

```python
import math

import jax
import jax.numpy as jnp
from jax import lax
from jax.sharding import PartitionSpec as P

HD = 128


epsilon = 1e-05
rope_base = 500000.0


def shifted(shard, axis, by):
    devices = lax.axis_size(axis)
    pairs = [(i, i + by) for i in range(devices) if 0 <= i + by < devices]
    return lax.ppermute(shard, axis, pairs)


def exchange_sum(blocks, axis, dim=0):
    devices = lax.axis_size(axis)
    me = lax.axis_index(axis)
    total = lax.dynamic_index_in_dim(blocks, me, axis=dim, keepdims=False).astype(jnp.float32)
    for by in range(1, devices):
        outgoing = lax.dynamic_index_in_dim(blocks, (me + by) % devices, axis=dim, keepdims=False)
        incoming = lax.ppermute(outgoing, axis, [(i, (i + by) % devices) for i in range(devices)])
        total = total + incoming.astype(jnp.float32)
    return total


def chip_pair_exchange_sum(blocks, axis):
    me = lax.axis_index(axis)
    pick = lambda index: lax.dynamic_index_in_dim(blocks, index, axis=0, keepdims=False)
    siblings = [(i, i ^ 1) for i in range(4)]
    for_pair = lax.ppermute(pick(me ^ 3), axis, siblings)
    pair = pick(me ^ 2).astype(jnp.float32) + for_pair.astype(jnp.float32)
    back = lax.ppermute(pair.astype(jnp.bfloat16), axis, [(i, i ^ 2) for i in range(4)])
    for_own = lax.ppermute(pick(me ^ 1), axis, siblings)
    own = pick(me).astype(jnp.float32) + for_own.astype(jnp.float32)
    return own + back.astype(jnp.float32)


def position_tables(document_ids, head_dim):
    seq_len = document_ids.shape[1]
    index = jnp.arange(seq_len, dtype=jnp.int32)
    earlier = (document_ids[:, None, :] < document_ids[:, :, None]).astype(jnp.int32)
    position = index[None, :] - jnp.sum(earlier, axis=2)
    half = head_dim // 2
    expo = jnp.arange(half, dtype=jnp.float32) * (2.0 / head_dim)
    freq = jnp.exp(expo * -math.log(rope_base))
    angle = position.astype(jnp.float32)[:, :, None] * freq
    same = document_ids[:, :, None] == document_ids[:, None, :]
    causal = index[:, None] >= index[None, :]
    visible = jnp.logical_and(same, causal[None])
    return (jnp.cos(angle), jnp.sin(angle), visible)


def rotate(vector, rot_cos, rot_sin, direction):
    half = vector.shape[-1] // 2
    first = vector[..., :half]
    second = vector[..., half:]
    return jnp.concatenate(
        [
            first * rot_cos - direction * second * rot_sin,
            second * rot_cos + direction * first * rot_sin,
        ],
        axis=-1,
    )


def normalize(rows, gain):
    values = rows.astype(jnp.float32)
    inverse = lax.rsqrt(jnp.mean(values * values, axis=-1, keepdims=True) + epsilon)
    unit_rows = values * inverse
    normed = (unit_rows * gain.astype(jnp.float32)).astype(jnp.bfloat16)
    return (inverse, unit_rows, normed)


def attention_forward(query_rot, key_rot, value_low, visible):
    scale = 1.0 / math.sqrt(HD)
    scores = (
        jnp.einsum("bqngd,bknd->bngqk", query_rot, key_rot, preferred_element_type=jnp.float32)
        * scale
    )
    expo = jnp.where(visible[:, None, None], jnp.exp(scores), 0.0)
    prob = expo / jnp.sum(expo, axis=-1, keepdims=True)
    prob_low = prob.astype(jnp.bfloat16)
    mixed = jnp.einsum("bngqk,bknd->bqngd", prob_low, value_low, preferred_element_type=jnp.float32)
    return (prob, prob_low, mixed.astype(jnp.bfloat16))


def attention_backward(grad_mixed, query_rot, key_rot, value_low, prob, prob_low, rot_cos, rot_sin):
    scale = 1.0 / math.sqrt(HD)
    grad_value = jnp.einsum(
        "bngqk,bqngd->bknd", prob_low, grad_mixed, preferred_element_type=jnp.float32
    )
    grad_prob = jnp.einsum(
        "bqngd,bknd->bngqk", grad_mixed, value_low, preferred_element_type=jnp.float32
    )
    grad_score = prob * (grad_prob - jnp.sum(grad_prob * prob, axis=-1, keepdims=True)) * scale
    score_low = grad_score.astype(jnp.bfloat16)
    grad_query = jnp.einsum(
        "bngqk,bknd->bqngd", score_low, key_rot, preferred_element_type=jnp.float32
    )
    grad_key = jnp.einsum(
        "bngqk,bqngd->bknd", score_low, query_rot, preferred_element_type=jnp.float32
    )
    grad_query = rotate(
        grad_query, rot_cos[:, :, None, None, :], rot_sin[:, :, None, None, :], -1.0
    )
    grad_key = rotate(grad_key, rot_cos[:, :, None, :], rot_sin[:, :, None, :], -1.0)
    return (
        grad_query.astype(jnp.bfloat16),
        grad_key.astype(jnp.bfloat16),
        grad_value.astype(jnp.bfloat16),
    )


def back_norm(grad_normed, unit_rows, inverse, gain, incoming):
    grad_unit = grad_normed * gain.astype(jnp.float32)
    branch = (
        grad_unit - unit_rows * jnp.mean(grad_unit * unit_rows, axis=-1, keepdims=True)
    ) * inverse
    return (incoming.astype(jnp.float32) + branch).astype(jnp.bfloat16)


def local(
    section_inputs,
    norm_gain,
    query_weight,
    key_weight,
    value_weight,
    output_weight,
    upstream_grad,
    document_ids,
):
    pipes = lax.axis_size("pipe")
    section = lax.axis_index("pipe")
    groups = lax.axis_size("dp")
    width = section_inputs.shape[2]
    seq_len = document_ids.shape[1]
    q_width = query_weight.shape[2]
    k_width = key_weight.shape[2]
    kv_local = k_width // HD
    group = q_width // k_width
    gain = norm_gain[0]
    w_query = query_weight[0]
    w_key = key_weight[0]
    w_value = value_weight[0]
    w_output = output_weight[0]
    rot_cos, rot_sin, visible = position_tables(document_ids, HD)
    last = pipes - 1
    inverse, unit_rows, normed_shard = normalize(section_inputs[0], gain)
    normed = lax.all_gather(normed_shard, "tensor", axis=0, tiled=True)
    incoming = jnp.where(section == last, upstream_grad, jnp.zeros_like(upstream_grad))
    query = jnp.dot(normed, w_query, preferred_element_type=jnp.float32).reshape(
        1, seq_len, kv_local, group, HD
    )
    keys = jnp.dot(normed, w_key, preferred_element_type=jnp.float32).reshape(
        1, seq_len, kv_local, HD
    )
    values = jnp.dot(normed, w_value, preferred_element_type=jnp.float32).reshape(
        1, seq_len, kv_local, HD
    )
    query_rot = rotate(
        query, rot_cos[:, :, None, None, :], rot_sin[:, :, None, None, :], 1.0
    ).astype(jnp.bfloat16)
    key_rot = rotate(keys, rot_cos[:, :, None, :], rot_sin[:, :, None, :], 1.0).astype(jnp.bfloat16)
    value_low = values.astype(jnp.bfloat16)
    prob, prob_low, mixed = attention_forward(query_rot, key_rot, value_low, visible)
    mixed_rows = lax.optimization_barrier(mixed.reshape(seq_len, q_width).T)

    def backward_turn(cotangent):
        grad_mixed = jnp.einsum(
            "sd,hd->sh", cotangent, w_output, preferred_element_type=jnp.float32
        )
        grad_mixed = grad_mixed.astype(jnp.bfloat16).reshape(1, seq_len, kv_local, group, HD)
        grad_query, grad_key, grad_value = attention_backward(
            grad_mixed, query_rot, key_rot, value_low, prob, prob_low, rot_cos, rot_sin
        )
        flat_query = grad_query.reshape(seq_len, q_width)
        flat_key = grad_key.reshape(seq_len, k_width)
        flat_value = grad_value.reshape(seq_len, k_width)
        return (flat_query, flat_key, flat_value)

    def project_back(flat_query, flat_key, flat_value):
        grad_normed = (
            jnp.einsum("sh,dh->sd", flat_query, w_query, preferred_element_type=jnp.float32)
            + jnp.einsum("sh,dh->sd", flat_key, w_key, preferred_element_type=jnp.float32)
            + jnp.einsum("sh,dh->sd", flat_value, w_value, preferred_element_type=jnp.float32)
        )
        return grad_normed.astype(jnp.bfloat16)

    def skipped_turn(cotangent):
        return (
            jnp.zeros((seq_len, q_width), jnp.bfloat16),
            jnp.zeros((seq_len, k_width), jnp.bfloat16),
            jnp.zeros((seq_len, k_width), jnp.bfloat16),
        )

    saved_query = jnp.zeros((seq_len, q_width), jnp.bfloat16)
    saved_key = jnp.zeros((seq_len, k_width), jnp.bfloat16)
    saved_value = jnp.zeros((seq_len, k_width), jnp.bfloat16)
    saved_cot = jnp.zeros((seq_len, width), jnp.bfloat16)
    saved_input = jnp.zeros_like(incoming)
    for turn in range(pipes):
        active = section == last - turn
        cotangent = lax.all_gather(incoming, "tensor", axis=0, tiled=True)
        flat_query, flat_key, flat_value = lax.cond(active, backward_turn, skipped_turn, cotangent)
        grad_normed = project_back(flat_query, flat_key, flat_value)
        tensors = lax.axis_size("tensor")
        grad_blocks = grad_normed.reshape(tensors, seq_len // tensors, width)
        if tensors == 4:
            summed = chip_pair_exchange_sum(grad_blocks, "tensor")
        else:
            summed = exchange_sum(grad_blocks, "tensor")
        result = back_norm(summed, unit_rows, inverse, gain, incoming)
        saved_query = jnp.where(active, flat_query, saved_query)
        saved_key = jnp.where(active, flat_key, saved_key)
        saved_value = jnp.where(active, flat_value, saved_value)
        saved_cot = jnp.where(active, cotangent, saved_cot)
        saved_input = jnp.where(active, result, saved_input)
        if turn + 1 < pipes:
            incoming = shifted(result, "pipe", -1)
    scale_out = 1.0 / math.sqrt(groups * seq_len)
    block = width // groups
    out_term = jnp.dot(mixed_rows, saved_cot, preferred_element_type=jnp.float32).astype(jnp.bfloat16)
    out_parts = lax.all_to_all(out_term.reshape(q_width, groups, block), "dp", 1, 1, tiled=True)
    output_grads = jnp.sum(out_parts.astype(jnp.float32), axis=1) * scale_out
    grads_qkv = jnp.concatenate([saved_query, saved_key, saved_value], axis=1)
    qkv_term = jnp.einsum(
        "sh,sjd->jhd",
        grads_qkv,
        normed.reshape(seq_len, groups, block),
        preferred_element_type=jnp.float32,
    ).astype(jnp.bfloat16)
    qkv_parts = lax.all_to_all(qkv_term, "dp", 0, 0, tiled=True)
    sums = jnp.sum(qkv_parts.astype(jnp.float32), axis=0).T * scale_out
    query_grads = sums[:, :q_width][None]
    key_grads = sums[:, q_width : q_width + k_width][None]
    value_grads = sums[:, q_width + k_width :][None]
    return (saved_input[None], query_grads, key_grads, value_grads, output_grads[None])


def solution(mesh):
    placed = (
        P("pipe", ("dp", "tensor"), None),
        P("pipe", None),
        P("pipe", None, "tensor"),
        P("pipe", None, "tensor"),
        P("pipe", None, "tensor"),
        P("pipe", "tensor", None),
        P(("dp", "tensor"), None),
        P("dp", None),
    )
    return jax.shard_map(
        local,
        mesh=mesh,
        in_specs=placed,
        out_specs=(
            P("pipe", ("dp", "tensor"), None),
            P("pipe", "dp", "tensor"),
            P("pipe", "dp", "tensor"),
            P("pipe", "dp", "tensor"),
            P("pipe", "tensor", "dp"),
        ),
        check_vma=False,
    )
```
